32 devices in a mesh: grp: 2 (over y), shot: 4 (over z), freq: 2 (over x), sub: 2 (over core).
Axes of the slice: x: 2, y: 2, z: 4, core: 2. Of those that a mesh axis runs over, the one named last changes fastest.
Arguments:
- downgoing: bfloat16 [2, 2, 6144, 1024], P(None, 'freq', ('grp', 'shot')), parts along dimension 2
- upgoing: bfloat16 [2, 2, 6144, 512], P(None, 'freq', ('grp', 'shot')), parts along dimension 2, may hold values from -448 to 448
- source_order: int32 [1024], P('grp'), parts along dimension 0, may hold values from 0 to 511, each once
Outputs:
- response: float32 [2, 2, 1024, 1024], P(None, 'freq', ('grp', 'shot', 'sub')), parts along dimension 2
The draws below stay inside these ranges and needn't reach their ends.
There are 2 independent parts, one for each index of `grp`. The reference program is written for one: setup_inputs(seed, part) draws one part's arguments, and reference() takes and returns one part's arrays. A program takes and returns all parts, laid end to end along the dimension named above; each array names one. Nothing has to cross between parts.
Inputs may be any that keep to these rules, and one draw needn't show every extreme that they name: `source_order`: each of the 512 columns appears exactly once.
All inputs are finite; a program needn't handle non-finite values.
Results may differ from the reference program's by a relative error of at most 0.012.
Values may be sent and summed in bfloat16 or wider, within the bound.
No kernel may reach another device: no remote copies, remote signals or barrier semaphores. Data moves between devices by JAX's collectives and lax.ppermute only.
A program may use at most 64 MiB of HBM per device.

```python
import math
import jax
import jax.numpy as jnp
from jax import lax

RECEIVERS = 1024
SOURCES = 512
SHOT_DEV = 768
SWEEPS = 6
SHOTS = 3072
FREQS = 2
N_SHOT = 4


def draw_downgoing(key, part):
    first_key, second_key, third_key, fourth_key = jax.random.split(key, 4)
    position = jnp.arange(SHOTS, dtype=jnp.float32) / SHOTS
    ramp = jnp.sqrt(jnp.exp(position * math.log(3.0)))
    shape = (2, FREQS, SHOTS, RECEIVERS)
    block_total = 16
    block_level = jax.random.uniform(third_key, (block_total,), jnp.float32, -0.25, 0.25)
    block_wide = jnp.repeat(block_level, RECEIVERS // block_total)
    rough_level = jax.random.uniform(fourth_key, (RECEIVERS,), jnp.float32, -0.5 * math.log(3.0), 0.5 * math.log(3.0))
    coupling = jnp.exp(block_wide + rough_level)
    base = jax.random.normal(first_key, shape, jnp.float32)
    jitter = jnp.exp(jax.random.uniform(second_key, (1, FREQS, SHOTS, 1), jnp.float32, 0.0, math.log(2.0)))
    return (base * ramp[None, None, :, None] * jitter * coupling[None, None, None, :]).astype(jnp.bfloat16)


def strengthened(array, rng, source, target, parts, factor):
    def block_of(dim):
        return (jnp.arange(array.shape[dim]) // (array.shape[dim] // parts)).reshape((-1,) + (1,) * (array.ndim - 1 - dim))

    first = jax.random.permutation(rng, parts)[block_of(target)]
    far = (block_of(target) + parts // 2) % parts
    return jnp.where((block_of(source) == first) | (block_of(source) == far), factor * array, array)


def steps_of(stream_key, extent, shards, least, largest):
    gain, own = 1.0, jax.random.fold_in(stream_key, 6)
    for dim, blocks in shards:
        draws = jnp.exp(jax.random.uniform(jax.random.fold_in(own, dim), (blocks,), jnp.float32, least / len(shards), largest / len(shards)))
        gain = gain * jnp.repeat(draws, extent[dim] // blocks).reshape([-1 if axis == dim else 1 for axis in range(len(extent))])
    return gain


def noise_with(key, extent, spread, reach, cuts, heavy, kind=jnp.bfloat16):
    result = spread * jax.random.normal(key, extent, jnp.float32)
    if cuts:
        result = result * steps_of(key, extent, cuts, -0.22, 0.18)
    return jnp.clip(strengthened(result, jax.random.fold_in(key, 3), *heavy), -reach, reach).astype(kind)


def setup_inputs(seed: int = 0, part: int = 0) -> dict:
    key_of = jax.random.split(jax.random.key(seed), 4)
    part_keys = jax.random.split(jax.random.fold_in(key_of[3], part), 4)
    return {
        "downgoing": draw_downgoing(jax.random.fold_in(jax.random.fold_in(key_of[3], part), 71), part),
        "upgoing": noise_with(part_keys[1], (2, FREQS, SHOTS, SOURCES), (SHOTS ** 0.5), 448.0, ((1, 2), (2, 4)), (2, 3, 4, 2.0)),
        "source_order": jax.random.permutation(part_keys[2], SOURCES).astype(jnp.int32),
    }


relaxation = 0.125
damping = 1.0


def complex_terms(left_factor, right):
    real = jnp.dot(left_factor[0].T, right[0], preferred_element_type=jnp.float32) + jnp.dot(left_factor[1].T, right[1], preferred_element_type=jnp.float32)
    imag = jnp.dot(left_factor[1].T, right[0], preferred_element_type=jnp.float32) - jnp.dot(left_factor[0].T, right[1], preferred_element_type=jnp.float32)
    return jnp.stack([real, imag])


def rounded_sum(total, term):
    narrow = lax.optimization_barrier(term.astype(jnp.bfloat16))
    return total + narrow.astype(jnp.float32)


def reference(downgoing, upgoing, source_order):
    chosen_all = jnp.take(upgoing, source_order, axis=3)
    results = []
    for freq_index in range(FREQS):
        recorded_trace = downgoing[:, freq_index]
        chosen = chosen_all[:, freq_index]
        power = jnp.sum(jnp.square(recorded_trace.astype(jnp.float32))) / RECEIVERS
        wave_blocks = jnp.transpose(recorded_trace.reshape(2, N_SHOT, SHOT_DEV, RECEIVERS), (1, 0, 2, 3))
        chosen_blocks = jnp.transpose(chosen.reshape(2, N_SHOT, SHOT_DEV, SOURCES), (1, 0, 2, 3))

        def accumulate(carry, blocks):
            gram, corr = carry
            wave_block, chosen_block = blocks
            gram = rounded_sum(gram, complex_terms(wave_block, wave_block))
            corr = rounded_sum(corr, complex_terms(chosen_block, wave_block))
            return (gram, corr), None

        start = (jnp.zeros((2, RECEIVERS, RECEIVERS), jnp.float32), jnp.zeros((2, SOURCES, RECEIVERS), jnp.float32))
        (gram, corr), unused = lax.scan(accumulate, start, (wave_blocks, chosen_blocks))
        scaled = (gram / power).astype(jnp.bfloat16)
        target = corr / power
        solution = jnp.zeros((2, SOURCES, RECEIVERS), jnp.float32)
        for sweep in range(SWEEPS):
            narrow = solution.astype(jnp.bfloat16)
            image_real = jnp.dot(narrow[0], scaled[0], preferred_element_type=jnp.float32) - jnp.dot(narrow[1], scaled[1], preferred_element_type=jnp.float32)
            image_imag = jnp.dot(narrow[0], scaled[1], preferred_element_type=jnp.float32) + jnp.dot(narrow[1], scaled[0], preferred_element_type=jnp.float32)
            image = jnp.stack([image_real, image_imag])
            solution = solution + relaxation * (target - image - damping * solution)
        results.append(solution)
    return jnp.stack(results, axis=1)
```

```python
import jax
import jax.numpy as jnp
from jax import lax
from jax.sharding import PartitionSpec as P

SWEEPS = 6


relaxation = 0.125
damping = 1.0


def stacked_left(factor):
    real_left = jnp.concatenate([factor[0], factor[1]], axis=1)
    imag_left = jnp.concatenate([factor[1], -factor[0]], axis=1)
    return jnp.stack([real_left, imag_left], axis=2)


def stacked_right(trace):
    return jnp.concatenate([trace[0], trace[1]], axis=1)


def sweep_whole(scaled, solution, target):
    for sweep in range(SWEEPS):
        narrow = solution.astype(jnp.bfloat16)
        real_real = jnp.einsum("qjc,qcr->qjr", narrow[0], scaled[0], preferred_element_type=jnp.float32)
        imag_imag = jnp.einsum("qjc,qcr->qjr", narrow[1], scaled[1], preferred_element_type=jnp.float32)
        real_imag = jnp.einsum("qjc,qcr->qjr", narrow[0], scaled[1], preferred_element_type=jnp.float32)
        imag_real = jnp.einsum("qjc,qcr->qjr", narrow[1], scaled[0], preferred_element_type=jnp.float32)
        image = jnp.stack([real_real - imag_imag, real_imag + imag_real])
        solution = solution + relaxation * (target - image - damping * solution)
    return solution


def per_device(downgoing, upgoing, source_order):
    shot_count = lax.axis_size("shot")
    core_count = lax.axis_size("sub")
    core_index = lax.axis_index("sub")
    receivers = downgoing.shape[3]
    freq_local = downgoing.shape[1]
    shot_local = downgoing.shape[2]
    sources = source_order.shape[0]
    source_local = sources // (shot_count * core_count)
    block = receivers // (shot_count * core_count)

    right = stacked_right(downgoing)

    columns = downgoing.reshape(2, freq_local, shot_local, shot_count, core_count, block)
    own_columns = lax.dynamic_slice_in_dim(columns, core_index, 1, 4)[:, :, :, :, 0]
    own_columns = own_columns.reshape(2, freq_local, shot_local, shot_count * block)
    gram_part = jnp.einsum(
        "qtpu,qto->qpuo", stacked_left(own_columns), right, preferred_element_type=jnp.float32
    )
    gram_part = gram_part.reshape(freq_local, 2, shot_count, block, receivers)
    gram_part = jnp.transpose(gram_part, (2, 0, 1, 3, 4)).astype(jnp.bfloat16)
    gram_rows = lax.psum_scatter(gram_part, "shot", scatter_dimension=0, tiled=True)
    across = lax.all_gather(gram_rows, "shot", axis=0, tiled=True)
    whole = lax.all_gather(across, "sub", axis=1, tiled=False)
    whole = jnp.transpose(whole, (3, 2, 0, 1, 4, 5)).reshape(2, freq_local, receivers, receivers)

    local_power = jnp.sum(jnp.square(downgoing.astype(jnp.float32)), axis=(0, 2, 3))
    power = jnp.sum(lax.all_gather(local_power, "shot", axis=0), axis=0) / receivers
    power_wide = power[None, :, None, None]

    corr_all = jnp.einsum(
        "qtpu,qto->uqpo", stacked_left(upgoing), right, preferred_element_type=jnp.float32
    )
    order_table = source_order.reshape(shot_count, core_count, source_local)
    own_order = lax.dynamic_slice_in_dim(order_table, core_index, 1, 1).reshape(-1)
    corr_part = jnp.take(corr_all, own_order, axis=0).astype(jnp.bfloat16)
    corr = lax.psum_scatter(corr_part, "shot", scatter_dimension=0, tiled=True).astype(jnp.float32)
    target = jnp.transpose(corr, (2, 1, 0, 3)) / power_wide

    scaled = (whole.astype(jnp.float32) / power_wide).astype(jnp.bfloat16)
    solution = jnp.zeros((2, freq_local, source_local, receivers), jnp.float32)
    return sweep_whole(scaled, solution, target)


def solution(mesh):
    return jax.shard_map(
        per_device,
        mesh=mesh,
        in_specs=(
            P(None, "freq", ("grp", "shot"), None),
            P(None, "freq", ("grp", "shot"), None),
            P("grp"),
        ),
        out_specs=P(None, "freq", ("grp", "shot", "sub"), None),
        check_vma=False,
    )
```

```python
import jax
import jax.numpy as jnp
from jax import lax
from jax.sharding import PartitionSpec as P

SWEEPS = 6


relaxation = 0.125
damping = 1.0


def stacked_left(factor):
    real_left = jnp.concatenate([factor[0], factor[1]], axis=1)
    imag_left = jnp.concatenate([factor[1], -factor[0]], axis=1)
    return jnp.stack([real_left, imag_left], axis=2)


def stacked_right(trace):
    return jnp.concatenate([trace[0], trace[1]], axis=1)


def sweep_whole(scaled, solution, target):
    for sweep in range(SWEEPS):
        narrow = solution.astype(jnp.bfloat16)
        real_real = jnp.einsum("qjc,qcr->qjr", narrow[0], scaled[0], preferred_element_type=jnp.float32)
        imag_imag = jnp.einsum("qjc,qcr->qjr", narrow[1], scaled[1], preferred_element_type=jnp.float32)
        real_imag = jnp.einsum("qjc,qcr->qjr", narrow[0], scaled[1], preferred_element_type=jnp.float32)
        imag_real = jnp.einsum("qjc,qcr->qjr", narrow[1], scaled[0], preferred_element_type=jnp.float32)
        image = jnp.stack([real_real - imag_imag, real_imag + imag_real])
        solution = solution + relaxation * (target - image - damping * solution)
    return solution


def per_device(downgoing, upgoing, source_order):
    shot_count = lax.axis_size("shot")
    core_count = lax.axis_size("sub")
    core_index = lax.axis_index("sub")
    receivers = downgoing.shape[3]
    freq_local = downgoing.shape[1]
    sources = source_order.shape[0]
    source_local = sources // (shot_count * core_count)
    block = receivers // (shot_count * core_count)

    right = stacked_right(downgoing)

    gram_full = jnp.einsum(
        "qtpu,qto->uqpo", stacked_left(downgoing), right, preferred_element_type=jnp.float32
    )
    gram_full = gram_full.reshape(shot_count, core_count, block, freq_local, 2, receivers)
    gram_part = lax.dynamic_slice_in_dim(gram_full, core_index, 1, 1)
    gram_part = gram_part.reshape(shot_count * block, freq_local, 2, receivers).astype(jnp.bfloat16)
    gram_rows = lax.psum_scatter(gram_part, "shot", scatter_dimension=0, tiled=True)

    local_power = jnp.sum(jnp.square(downgoing.astype(jnp.float32)), axis=(0, 2, 3))
    power = lax.psum(local_power, "shot") / receivers

    corr_all = jnp.einsum(
        "qtpu,qto->uqpo", stacked_left(upgoing), right, preferred_element_type=jnp.float32
    )
    order_table = source_order.reshape(shot_count, core_count, source_local)
    own_order = lax.dynamic_slice_in_dim(order_table, core_index, 1, 1).reshape(-1)
    corr_part = jnp.take(corr_all, own_order, axis=0).astype(jnp.bfloat16)

    gram_rows, corr_part, power = lax.optimization_barrier((gram_rows, corr_part, power))
    power_wide = power[None, :, None, None]

    across = lax.all_gather(gram_rows, "shot", axis=0, tiled=True)
    across = across.reshape(shot_count, block, freq_local, 2, receivers)
    whole = lax.all_gather(across, "sub", axis=1, tiled=False)
    whole = whole.reshape(receivers, freq_local, 2, receivers)
    whole = jnp.transpose(whole, (2, 1, 0, 3))

    corr = lax.psum_scatter(corr_part, "shot", scatter_dimension=0, tiled=True).astype(jnp.float32)
    target = jnp.transpose(corr, (2, 1, 0, 3)) / power_wide

    scaled = (whole.astype(jnp.float32) / power_wide).astype(jnp.bfloat16)
    solution = jnp.zeros((2, freq_local, source_local, receivers), jnp.float32)
    return sweep_whole(scaled, solution, target)


def solution(mesh):
    return jax.shard_map(
        per_device,
        mesh=mesh,
        in_specs=(
            P(None, "freq", ("grp", "shot"), None),
            P(None, "freq", ("grp", "shot"), None),
            P("grp"),
        ),
        out_specs=P(None, "freq", ("grp", "shot", "sub"), None),
        check_vma=False,
    )
```

```python
import jax
import jax.numpy as jnp
from jax import lax
from jax.sharding import PartitionSpec as P

SWEEPS = 6


relaxation = 0.125
damping = 1.0


def stacked_left(factor):
    real_left = jnp.concatenate([factor[0], factor[1]], axis=1)
    imag_left = jnp.concatenate([factor[1], -factor[0]], axis=1)
    return jnp.stack([real_left, imag_left], axis=2)


def stacked_right(trace):
    return jnp.concatenate([trace[0], trace[1]], axis=1)


def sweep_whole(scaled, solution, target):
    for sweep in range(SWEEPS):
        narrow = solution.astype(jnp.bfloat16)
        real_real = jnp.einsum("qjc,qcr->qjr", narrow[0], scaled[0], preferred_element_type=jnp.float32)
        imag_imag = jnp.einsum("qjc,qcr->qjr", narrow[1], scaled[1], preferred_element_type=jnp.float32)
        real_imag = jnp.einsum("qjc,qcr->qjr", narrow[0], scaled[1], preferred_element_type=jnp.float32)
        imag_real = jnp.einsum("qjc,qcr->qjr", narrow[1], scaled[0], preferred_element_type=jnp.float32)
        image = jnp.stack([real_real - imag_imag, real_imag + imag_real])
        solution = solution + relaxation * (target - image - damping * solution)
    return solution


def strip_partials(gram_full, shot_count, core_count, core_index, rows_each, tile, span):
    receivers = gram_full.shape[0]
    rows = gram_full.reshape(shot_count, core_count, rows_each, *gram_full.shape[1:])
    rows = lax.dynamic_slice_in_dim(rows, core_index, 1, 1)[:, 0].astype(jnp.bfloat16)
    doubled = jnp.concatenate([rows, rows], axis=-1)
    windows = []
    for k in range(shot_count):
        start = ((k * core_count + core_index) * rows_each // tile) * tile
        windows.append(lax.dynamic_slice_in_dim(doubled[k], start, span, axis=-1))
    return jnp.stack(windows).reshape(shot_count * rows_each, *gram_full.shape[1:3], span)


def rebuild_gram(strips, groups, block):
    half = groups // 2
    freq_local = strips.shape[2]
    pieces = strips.reshape(groups, block, freq_local, 2, half + 1, block)
    direct = [pieces[:, :, :, :, offset, :] for offset in range(half + 1)]
    mirrored = []
    for offset in range(half + 1, groups):
        back = groups - offset
        source = pieces[:, :, :, :, back, :]
        flipped = jnp.transpose(source, (0, 4, 2, 3, 1))
        flipped = jnp.stack([flipped[:, :, :, 0], -flipped[:, :, :, 1]], axis=3)
        mirrored.append(jnp.roll(flipped, back, axis=0))
    cyclic = jnp.stack(direct + mirrored, axis=1)
    doubled = jnp.concatenate([cyclic, cyclic], axis=1)
    flat = doubled.reshape(2 * groups * groups, *doubled.shape[2:])
    skewed = flat[groups : groups + groups * (2 * groups - 1)]
    blocks = skewed.reshape(groups, 2 * groups - 1, *doubled.shape[2:])[:, :groups]
    blocks = jnp.transpose(blocks, (4, 3, 0, 2, 1, 5))
    return blocks.reshape(2, freq_local, groups * block, groups * block)


def per_device(downgoing, upgoing, source_order):
    shot_count = lax.axis_size("shot")
    core_count = lax.axis_size("sub")
    core_index = lax.axis_index("sub")
    receivers = downgoing.shape[3]
    freq_local = downgoing.shape[1]
    sources = source_order.shape[0]
    groups = shot_count * core_count
    source_local = sources // groups
    rows_each = receivers // groups
    tiles = 8 if groups % 8 == 0 else groups
    tile = receivers // tiles
    span = (tiles // 2 + 1) * tile

    right = stacked_right(downgoing)

    gram_full = jnp.einsum(
        "qtpu,qto->uqpo", stacked_left(downgoing), right, preferred_element_type=jnp.float32
    )
    gram_part = strip_partials(gram_full, shot_count, core_count, core_index, rows_each, tile, span)
    gram_strip = lax.psum_scatter(gram_part, "shot", scatter_dimension=0, tiled=True)

    local_power = jnp.sum(jnp.square(downgoing.astype(jnp.float32)), axis=(0, 2, 3))
    power = lax.psum(local_power, "shot") / receivers

    corr_all = jnp.einsum(
        "qtpu,qto->uqpo", stacked_left(upgoing), right, preferred_element_type=jnp.float32
    )
    order_table = source_order.reshape(shot_count, core_count, source_local)
    own_order = lax.dynamic_slice_in_dim(order_table, core_index, 1, 1).reshape(-1)
    corr_part = jnp.take(corr_all, own_order, axis=0).astype(jnp.bfloat16)

    gram_strip, corr_part, power = lax.optimization_barrier((gram_strip, corr_part, power))
    power_wide = power[None, :, None, None]

    across = lax.all_gather(gram_strip, "shot", axis=0, tiled=True)
    across = across.reshape(shot_count, rows_each, freq_local, 2, span)
    if core_count == 2:
        other = lax.ppermute(across, "sub", perm=[(0, 1), (1, 0)])
        first = jnp.where(core_index == 0, across, other)
        second = jnp.where(core_index == 0, other, across)
        strips = jnp.stack([first, second], axis=1)
    else:
        strips = lax.all_gather(across, "sub", axis=1, tiled=False)
    strips = strips.reshape(tiles, tile, freq_local, 2, span)
    whole = rebuild_gram(strips, tiles, tile)

    corr = lax.psum_scatter(corr_part, "shot", scatter_dimension=0, tiled=True).astype(jnp.float32)
    target = jnp.transpose(corr, (2, 1, 0, 3)) / power_wide

    scaled = (whole.astype(jnp.float32) / power_wide).astype(jnp.bfloat16)
    solution = jnp.zeros((2, freq_local, source_local, receivers), jnp.float32)
    return sweep_whole(scaled, solution, target)


def solution(mesh):
    return jax.shard_map(
        per_device,
        mesh=mesh,
        in_specs=(
            P(None, "freq", ("grp", "shot"), None),
            P(None, "freq", ("grp", "shot"), None),
            P("grp"),
        ),
        out_specs=P(None, "freq", ("grp", "shot", "sub"), None),
        check_vma=False,
    )
```

```python
import jax
import jax.numpy as jnp
from jax import lax
from jax.sharding import PartitionSpec as P

SWEEPS = 6


relaxation = 0.125
damping = 1.0


def stacked_left(factor):
    real_left = jnp.concatenate([factor[0], factor[1]], axis=1)
    imag_left = jnp.concatenate([factor[1], -factor[0]], axis=1)
    return jnp.stack([real_left, imag_left], axis=2)


def stacked_right(trace):
    return jnp.concatenate([trace[0], trace[1]], axis=1)


def sweep_whole(scaled, solution, target):
    for sweep in range(SWEEPS):
        narrow = solution.astype(jnp.bfloat16)
        real_real = jnp.einsum("qjc,qcr->qjr", narrow[0], scaled[0], preferred_element_type=jnp.float32)
        imag_imag = jnp.einsum("qjc,qcr->qjr", narrow[1], scaled[1], preferred_element_type=jnp.float32)
        real_imag = jnp.einsum("qjc,qcr->qjr", narrow[0], scaled[1], preferred_element_type=jnp.float32)
        imag_real = jnp.einsum("qjc,qcr->qjr", narrow[1], scaled[0], preferred_element_type=jnp.float32)
        image = jnp.stack([real_real - imag_imag, real_imag + imag_real])
        solution = solution + relaxation * (target - image - damping * solution)
    return solution


def strip_partials(gram_full, shot_count, core_count, core_index, rows_each, tile, span):
    receivers = gram_full.shape[0]
    rows = gram_full.reshape(shot_count, core_count, rows_each, *gram_full.shape[1:])
    rows = lax.dynamic_slice_in_dim(rows, core_index, 1, 1)[:, 0].astype(jnp.bfloat16)
    doubled = jnp.concatenate([rows, rows], axis=-1)
    windows = []
    for k in range(shot_count):
        start = ((k * core_count + core_index) * rows_each // tile) * tile
        windows.append(lax.dynamic_slice_in_dim(doubled[k], start, span, axis=-1))
    return jnp.stack(windows).reshape(shot_count * rows_each, *gram_full.shape[1:3], span)


def rebuild_gram(strips, tiles, tile):
    freq_local = strips.shape[1]
    receivers = tiles * tile
    span = strips.shape[-1]
    padded = jnp.pad(strips, [(0, 0)] * 3 + [(0, receivers - span)])
    padded = padded.reshape(tiles, tile, freq_local, 2, receivers)
    upper = jnp.stack([jnp.roll(padded[a], a * tile, axis=-1) for a in range(tiles)])
    upper = jnp.transpose(upper, (3, 2, 0, 1, 4)).reshape(2, freq_local, receivers, receivers)
    mirror = jnp.swapaxes(upper, 2, 3)
    mirror = jnp.stack([mirror[0], -mirror[1]])
    row_tile = lax.broadcasted_iota(jnp.int32, (receivers, receivers), 0) // tile
    col_tile = lax.broadcasted_iota(jnp.int32, (receivers, receivers), 1) // tile
    direct = (col_tile - row_tile) % tiles <= tiles // 2
    return jnp.where(direct, upper, mirror)


def per_device(downgoing, upgoing, source_order):
    shot_count = lax.axis_size("shot")
    core_count = lax.axis_size("sub")
    core_index = lax.axis_index("sub")
    receivers = downgoing.shape[3]
    freq_local = downgoing.shape[1]
    sources = source_order.shape[0]
    groups = shot_count * core_count
    source_local = sources // groups
    rows_each = receivers // groups
    tiles = 8 if groups % 8 == 0 else groups
    tile = receivers // tiles
    span = (tiles // 2 + 1) * tile

    right = stacked_right(downgoing)

    gram_full = jnp.einsum(
        "qtpu,qto->uqpo", stacked_left(downgoing), right, preferred_element_type=jnp.float32
    )
    gram_part = strip_partials(gram_full, shot_count, core_count, core_index, rows_each, tile, span)
    gram_strip = lax.psum_scatter(gram_part, "shot", scatter_dimension=0, tiled=True)

    local_power = jnp.sum(jnp.square(downgoing.astype(jnp.float32)), axis=(0, 2, 3))
    power = lax.psum(local_power, "shot") / receivers

    corr_all = jnp.einsum(
        "qtpu,qto->uqpo", stacked_left(upgoing), right, preferred_element_type=jnp.float32
    )
    order_table = source_order.reshape(shot_count, core_count, source_local)
    own_order = lax.dynamic_slice_in_dim(order_table, core_index, 1, 1).reshape(-1)
    corr_part = jnp.take(corr_all, own_order, axis=0).astype(jnp.bfloat16)

    gram_strip, corr_part, power = lax.optimization_barrier((gram_strip, corr_part, power))
    power_wide = power[None, :, None, None]

    across = lax.all_gather(gram_strip, "shot", axis=0, tiled=True)
    across = across.reshape(shot_count, rows_each, freq_local, 2, span)
    if core_count == 2:
        other = lax.ppermute(across, "sub", perm=[(0, 1), (1, 0)])
        first = jnp.where(core_index == 0, across, other)
        second = jnp.where(core_index == 0, other, across)
        strips = jnp.stack([first, second], axis=1)
    else:
        strips = lax.all_gather(across, "sub", axis=1, tiled=False)
    strips = strips.reshape(receivers, freq_local, 2, span)
    whole = rebuild_gram(strips, tiles, tile)

    corr = lax.psum_scatter(corr_part, "shot", scatter_dimension=0, tiled=True).astype(jnp.float32)
    target = jnp.transpose(corr, (2, 1, 0, 3)) / power_wide

    scaled = (whole.astype(jnp.float32) / power_wide).astype(jnp.bfloat16)
    solution = jnp.zeros((2, freq_local, source_local, receivers), jnp.float32)
    return sweep_whole(scaled, solution, target)


def solution(mesh):
    return jax.shard_map(
        per_device,
        mesh=mesh,
        in_specs=(
            P(None, "freq", ("grp", "shot"), None),
            P(None, "freq", ("grp", "shot"), None),
            P("grp"),
        ),
        out_specs=P(None, "freq", ("grp", "shot", "sub"), None),
        check_vma=False,
    )
```

```python
import jax
import jax.numpy as jnp
from jax import lax
from jax.experimental import pallas as pl
from jax.sharding import PartitionSpec as P

SWEEPS = 6


relaxation = 0.125
damping = 1.0


def stacked_left(factor):
    real_left = jnp.concatenate([factor[0], factor[1]], axis=1)
    imag_left = jnp.concatenate([factor[1], -factor[0]], axis=1)
    return jnp.stack([real_left, imag_left], axis=2)


def stacked_right(trace):
    return jnp.concatenate([trace[0], trace[1]], axis=1)


def sweep_kernel(weight_ref, target_ref, out_ref):
    target = target_ref[...]
    solution = jnp.zeros_like(target)
    for sweep in range(SWEEPS):
        narrow = solution.astype(jnp.bfloat16)
        image = jnp.dot(narrow, weight_ref[...], preferred_element_type=jnp.float32)
        solution = solution + relaxation * (target - image - damping * solution)
    out_ref[...] = solution


def sweep_whole(scaled, target):
    receivers = target.shape[-1]
    results = []
    for freq in range(target.shape[1]):
        real, imag = scaled[0, freq], scaled[1, freq]
        weight = jnp.concatenate(
            [jnp.concatenate([real, imag], axis=1), jnp.concatenate([-imag, real], axis=1)], axis=0
        )
        stacked = jnp.concatenate([target[0, freq], target[1, freq]], axis=1)
        response = pl.pallas_call(
            sweep_kernel,
            out_shape=jax.ShapeDtypeStruct(stacked.shape, jnp.float32),
        )(weight, stacked)
        results.append(jnp.stack([response[:, :receivers], response[:, receivers:]]))
    return jnp.stack(results, axis=1)


def strip_partials(gram_full, shot_count, core_count, core_index, rows_each, tile, span):
    receivers = gram_full.shape[0]
    rows = gram_full.reshape(shot_count, core_count, rows_each, *gram_full.shape[1:])
    rows = lax.dynamic_slice_in_dim(rows, core_index, 1, 1)[:, 0].astype(jnp.bfloat16)
    doubled = jnp.concatenate([rows, rows], axis=-1)
    windows = []
    for k in range(shot_count):
        start = ((k * core_count + core_index) * rows_each // tile) * tile
        windows.append(lax.dynamic_slice_in_dim(doubled[k], start, span, axis=-1))
    return jnp.stack(windows).reshape(shot_count * rows_each, *gram_full.shape[1:3], span)


def rebuild_gram(strips, tiles, tile):
    freq_local = strips.shape[1]
    receivers = tiles * tile
    span = strips.shape[-1]
    padded = jnp.pad(strips, [(0, 0)] * 3 + [(0, receivers - span)])
    padded = padded.reshape(tiles, tile, freq_local, 2, receivers)
    upper = jnp.stack([jnp.roll(padded[a], a * tile, axis=-1) for a in range(tiles)])
    upper = jnp.transpose(upper, (3, 2, 0, 1, 4)).reshape(2, freq_local, receivers, receivers)
    mirror = jnp.swapaxes(upper, 2, 3)
    mirror = jnp.stack([mirror[0], -mirror[1]])
    row_tile = lax.broadcasted_iota(jnp.int32, (receivers, receivers), 0) // tile
    col_tile = lax.broadcasted_iota(jnp.int32, (receivers, receivers), 1) // tile
    direct = (col_tile - row_tile) % tiles <= tiles // 2
    return jnp.where(direct, upper, mirror)


def per_device(downgoing, upgoing, source_order):
    shot_count = lax.axis_size("shot")
    core_count = lax.axis_size("sub")
    core_index = lax.axis_index("sub")
    receivers = downgoing.shape[3]
    freq_local = downgoing.shape[1]
    sources = source_order.shape[0]
    groups = shot_count * core_count
    source_local = sources // groups
    rows_each = receivers // groups
    tiles = 8 if groups % 8 == 0 else groups
    tile = receivers // tiles
    span = (tiles // 2 + 1) * tile

    right = stacked_right(downgoing)

    gram_full = jnp.einsum(
        "qtpu,qto->uqpo", stacked_left(downgoing), right, preferred_element_type=jnp.float32
    )
    gram_part = strip_partials(gram_full, shot_count, core_count, core_index, rows_each, tile, span)
    gram_strip = lax.psum_scatter(gram_part, "shot", scatter_dimension=0, tiled=True)

    local_power = jnp.sum(jnp.square(downgoing.astype(jnp.float32)), axis=(0, 2, 3))
    power = lax.psum(local_power, "shot") / receivers

    corr_all = jnp.einsum(
        "qtpu,qto->uqpo", stacked_left(upgoing), right, preferred_element_type=jnp.float32
    )
    order_table = source_order.reshape(shot_count, core_count, source_local)
    own_order = lax.dynamic_slice_in_dim(order_table, core_index, 1, 1).reshape(-1)
    corr_part = jnp.take(corr_all, own_order, axis=0).astype(jnp.bfloat16)

    gram_strip, corr_part, power = lax.optimization_barrier((gram_strip, corr_part, power))
    power_wide = power[None, :, None, None]

    across = lax.all_gather(gram_strip, "shot", axis=0, tiled=True)
    across = across.reshape(shot_count, rows_each, freq_local, 2, span)
    if core_count == 2:
        other = lax.ppermute(across, "sub", perm=[(0, 1), (1, 0)])
        first = jnp.where(core_index == 0, across, other)
        second = jnp.where(core_index == 0, other, across)
        strips = jnp.stack([first, second], axis=1)
    else:
        strips = lax.all_gather(across, "sub", axis=1, tiled=False)
    strips = strips.reshape(receivers, freq_local, 2, span)
    whole = rebuild_gram(strips, tiles, tile)

    corr = lax.psum_scatter(corr_part, "shot", scatter_dimension=0, tiled=True).astype(jnp.float32)
    target = jnp.transpose(corr, (2, 1, 0, 3)) / power_wide

    scaled = (whole.astype(jnp.float32) / power_wide).astype(jnp.bfloat16)
    return sweep_whole(scaled, target)


def solution(mesh):
    return jax.shard_map(
        per_device,
        mesh=mesh,
        in_specs=(
            P(None, "freq", ("grp", "shot"), None),
            P(None, "freq", ("grp", "shot"), None),
            P("grp"),
        ),
        out_specs=P(None, "freq", ("grp", "shot", "sub"), None),
        check_vma=False,
    )
```

```python
import jax
import jax.numpy as jnp
from jax import lax
from jax.sharding import PartitionSpec as P

SWEEPS = 6


relaxation = 0.125
damping = 1.0


def stacked_rows(factor):
    real_left = jnp.concatenate([factor[0], factor[1]], axis=1)
    imag_left = jnp.concatenate([factor[1], -factor[0]], axis=1)
    return jnp.swapaxes(jnp.stack([real_left, imag_left], axis=1), 2, 3)


def stacked_left(factor):
    real_left = jnp.concatenate([factor[0], factor[1]], axis=1)
    imag_left = jnp.concatenate([factor[1], -factor[0]], axis=1)
    return jnp.stack([real_left, imag_left], axis=2)


def stacked_right(trace):
    return jnp.concatenate([trace[0], trace[1]], axis=1)


def sweep_whole(scaled, solution, target):
    for sweep in range(SWEEPS):
        narrow = solution.astype(jnp.bfloat16)
        real_real = jnp.einsum("qjc,qcr->qjr", narrow[0], scaled[0], preferred_element_type=jnp.float32)
        imag_imag = jnp.einsum("qjc,qcr->qjr", narrow[1], scaled[1], preferred_element_type=jnp.float32)
        real_imag = jnp.einsum("qjc,qcr->qjr", narrow[0], scaled[1], preferred_element_type=jnp.float32)
        imag_real = jnp.einsum("qjc,qcr->qjr", narrow[1], scaled[0], preferred_element_type=jnp.float32)
        image = jnp.stack([real_real - imag_imag, real_imag + imag_real])
        solution = solution + relaxation * (target - image - damping * solution)
    return solution


def strip_partials(rows, shot_count, core_count, core_index, rows_each, tile, span):
    rows = rows.astype(jnp.bfloat16)
    doubled = jnp.concatenate([rows, rows], axis=-1)
    windows = []
    for k in range(shot_count):
        start = ((k * core_count + core_index) * rows_each // tile) * tile
        windows.append(lax.dynamic_slice_in_dim(doubled[k], start, span, axis=-1))
    return jnp.stack(windows).reshape(shot_count * rows_each, *rows.shape[2:4], span)


def rebuild_gram(strips, tiles, tile):
    freq_local = strips.shape[1]
    receivers = tiles * tile
    span = strips.shape[-1]
    padded = jnp.pad(strips, [(0, 0)] * 3 + [(0, receivers - span)])
    padded = padded.reshape(tiles, tile, freq_local, 2, receivers)
    upper = jnp.stack([jnp.roll(padded[a], a * tile, axis=-1) for a in range(tiles)])
    upper = jnp.transpose(upper, (3, 2, 0, 1, 4)).reshape(2, freq_local, receivers, receivers)
    mirror = jnp.swapaxes(upper, 2, 3)
    mirror = jnp.stack([mirror[0], -mirror[1]])
    row_tile = lax.broadcasted_iota(jnp.int32, (receivers, receivers), 0) // tile
    col_tile = lax.broadcasted_iota(jnp.int32, (receivers, receivers), 1) // tile
    direct = (col_tile - row_tile) % tiles <= tiles // 2
    return jnp.where(direct, upper, mirror)


def per_device(downgoing, upgoing, source_order):
    shot_count = lax.axis_size("shot")
    core_count = lax.axis_size("sub")
    core_index = lax.axis_index("sub")
    receivers = downgoing.shape[3]
    freq_local = downgoing.shape[1]
    sources = source_order.shape[0]
    groups = shot_count * core_count
    source_local = sources // groups
    rows_each = receivers // groups
    tiles = 8 if groups % 8 == 0 else groups
    tile = receivers // tiles
    span = (tiles // 2 + 1) * tile

    right = stacked_right(downgoing)

    left = stacked_rows(downgoing).reshape(freq_local, 2, shot_count, core_count, rows_each, -1)
    left = lax.dynamic_slice_in_dim(left, core_index, 1, 3)[:, :, :, 0]
    gram_rows = jnp.einsum("qpkit,qto->kiqpo", left, right, preferred_element_type=jnp.float32)
    gram_part = strip_partials(gram_rows, shot_count, core_count, core_index, rows_each, tile, span)
    gram_strip = lax.psum_scatter(gram_part, "shot", scatter_dimension=0, tiled=True)

    local_power = jnp.sum(jnp.square(downgoing.astype(jnp.float32)), axis=(0, 2, 3))
    power = lax.psum(local_power, "shot") / receivers
    gram_strip, power = lax.optimization_barrier((gram_strip, power))
    power_wide = power[None, :, None, None]

    across = lax.all_gather(gram_strip, "shot", axis=0, tiled=True)
    across = across.reshape(shot_count, rows_each, freq_local, 2, span)

    corr_all = jnp.einsum(
        "qtpu,qto->uqpo", stacked_left(upgoing), right, preferred_element_type=jnp.float32
    )
    order_table = source_order.reshape(shot_count, core_count, source_local)
    own_order = lax.dynamic_slice_in_dim(order_table, core_index, 1, 1).reshape(-1)
    corr_part = jnp.take(corr_all, own_order, axis=0).astype(jnp.bfloat16)
    across, corr_part = lax.optimization_barrier((across, corr_part))

    if core_count == 2:
        other = lax.ppermute(across, "sub", perm=[(0, 1), (1, 0)])
        first = jnp.where(core_index == 0, across, other)
        second = jnp.where(core_index == 0, other, across)
        strips = jnp.stack([first, second], axis=1)
    else:
        strips = lax.all_gather(across, "sub", axis=1, tiled=False)
    strips = strips.reshape(receivers, freq_local, 2, span)
    whole = rebuild_gram(strips, tiles, tile)

    corr = lax.psum_scatter(corr_part, "shot", scatter_dimension=0, tiled=True).astype(jnp.float32)
    target = jnp.transpose(corr, (2, 1, 0, 3)) / power_wide

    scaled = (whole.astype(jnp.float32) / power_wide).astype(jnp.bfloat16)
    solution = jnp.zeros((2, freq_local, source_local, receivers), jnp.float32)
    return sweep_whole(scaled, solution, target)


def solution(mesh):
    return jax.shard_map(
        per_device,
        mesh=mesh,
        in_specs=(
            P(None, "freq", ("grp", "shot"), None),
            P(None, "freq", ("grp", "shot"), None),
            P("grp"),
        ),
        out_specs=P(None, "freq", ("grp", "shot", "sub"), None),
        check_vma=False,
    )
```

```python
import jax
import jax.numpy as jnp
from jax import lax
from jax.sharding import PartitionSpec as P

SWEEPS = 6


relaxation = 0.125
damping = 1.0


def stacked_rows(factor):
    real_left = jnp.concatenate([factor[0], factor[1]], axis=1)
    imag_left = jnp.concatenate([factor[1], -factor[0]], axis=1)
    return jnp.swapaxes(jnp.stack([real_left, imag_left], axis=1), 2, 3)


def stacked_left(factor):
    real_left = jnp.concatenate([factor[0], factor[1]], axis=1)
    imag_left = jnp.concatenate([factor[1], -factor[0]], axis=1)
    return jnp.stack([real_left, imag_left], axis=2)


def stacked_right(trace):
    return jnp.concatenate([trace[0], trace[1]], axis=1)


def sweep_whole(scaled, solution, target):
    for sweep in range(SWEEPS):
        narrow = solution.astype(jnp.bfloat16)
        real_real = jnp.einsum("qjc,qcr->qjr", narrow[0], scaled[0], preferred_element_type=jnp.float32)
        imag_imag = jnp.einsum("qjc,qcr->qjr", narrow[1], scaled[1], preferred_element_type=jnp.float32)
        real_imag = jnp.einsum("qjc,qcr->qjr", narrow[0], scaled[1], preferred_element_type=jnp.float32)
        imag_real = jnp.einsum("qjc,qcr->qjr", narrow[1], scaled[0], preferred_element_type=jnp.float32)
        image = jnp.stack([real_real - imag_imag, real_imag + imag_real])
        solution = solution + relaxation * (target - image - damping * solution)
    return solution


def strip_partials(rows, shot_count, core_count, core_index, rows_each, tile, span):
    rows = rows.astype(jnp.bfloat16)
    doubled = jnp.concatenate([rows, rows], axis=-1)
    windows = []
    for k in range(shot_count):
        start = ((k * core_count + core_index) * rows_each // tile) * tile
        windows.append(lax.dynamic_slice_in_dim(doubled[k], start, span, axis=-1))
    return jnp.stack(windows).reshape(shot_count * rows_each, *rows.shape[2:4], span)


def rebuild_gram(strips, tiles, tile):
    freq_local = strips.shape[1]
    receivers = tiles * tile
    span = strips.shape[-1]
    padded = jnp.pad(strips, [(0, 0)] * 3 + [(0, receivers - span)])
    padded = padded.reshape(tiles, tile, freq_local, 2, receivers)
    upper = jnp.stack([jnp.roll(padded[a], a * tile, axis=-1) for a in range(tiles)])
    upper = jnp.transpose(upper, (3, 2, 0, 1, 4)).reshape(2, freq_local, receivers, receivers)
    mirror = jnp.swapaxes(upper, 2, 3)
    mirror = jnp.stack([mirror[0], -mirror[1]])
    row_tile = lax.broadcasted_iota(jnp.int32, (receivers, receivers), 0) // tile
    col_tile = lax.broadcasted_iota(jnp.int32, (receivers, receivers), 1) // tile
    direct = (col_tile - row_tile) % tiles <= tiles // 2
    return jnp.where(direct, upper, mirror)


def per_device(downgoing, upgoing, source_order):
    shot_count = lax.axis_size("shot")
    core_count = lax.axis_size("sub")
    core_index = lax.axis_index("sub")
    receivers = downgoing.shape[3]
    freq_local = downgoing.shape[1]
    sources = source_order.shape[0]
    groups = shot_count * core_count
    source_local = sources // groups
    rows_each = receivers // groups
    tiles = 8 if groups % 8 == 0 else groups
    tile = receivers // tiles
    span = (tiles // 2 + 1) * tile

    right = stacked_right(downgoing)

    left = stacked_rows(downgoing).reshape(freq_local, 2, shot_count, core_count, rows_each, -1)
    left = lax.dynamic_slice_in_dim(left, core_index, 1, 3)[:, :, :, 0]
    gram_rows = jnp.einsum("qpkit,qto->kiqpo", left, right, preferred_element_type=jnp.float32)
    gram_part = strip_partials(gram_rows, shot_count, core_count, core_index, rows_each, tile, span)
    gram_strip = lax.psum_scatter(gram_part, "shot", scatter_dimension=0, tiled=True)

    local_power = jnp.sum(jnp.square(downgoing.astype(jnp.float32)), axis=(0, 2, 3))
    power = lax.psum(local_power, "shot") / receivers

    corr_all = jnp.einsum(
        "qtpu,qto->uqpo", stacked_left(upgoing), right, preferred_element_type=jnp.float32
    )
    order_table = source_order.reshape(shot_count, core_count, source_local)
    own_order = lax.dynamic_slice_in_dim(order_table, core_index, 1, 1).reshape(-1)
    corr_part = jnp.take(corr_all, own_order, axis=0).astype(jnp.bfloat16)

    gram_strip, power, corr_part = lax.optimization_barrier((gram_strip, power, corr_part))
    power_wide = power[None, :, None, None]

    shot_index = lax.axis_index("shot")
    corr_blocks = corr_part.reshape(shot_count, source_local, *corr_part.shape[1:])
    corr = lax.dynamic_index_in_dim(corr_blocks, shot_index, 0, keepdims=False).astype(jnp.float32)
    for shift in range(1, shot_count):
        outgoing = lax.dynamic_index_in_dim(corr_blocks, (shot_index + shift) % shot_count, 0, keepdims=False)
        pairs = [(k, (k + shift) % shot_count) for k in range(shot_count)]
        corr = corr + lax.ppermute(outgoing, "shot", perm=pairs).astype(jnp.float32)

    across = lax.all_gather(gram_strip, "shot", axis=0, tiled=True)
    across = across.reshape(shot_count, rows_each, freq_local, 2, span)

    if core_count == 2:
        other = lax.ppermute(across, "sub", perm=[(0, 1), (1, 0)])
        first = jnp.where(core_index == 0, across, other)
        second = jnp.where(core_index == 0, other, across)
        strips = jnp.stack([first, second], axis=1)
    else:
        strips = lax.all_gather(across, "sub", axis=1, tiled=False)
    strips = strips.reshape(receivers, freq_local, 2, span)
    whole = rebuild_gram(strips, tiles, tile)

    target = jnp.transpose(corr, (2, 1, 0, 3)) / power_wide

    scaled = (whole.astype(jnp.float32) / power_wide).astype(jnp.bfloat16)
    solution = jnp.zeros((2, freq_local, source_local, receivers), jnp.float32)
    return sweep_whole(scaled, solution, target)


def solution(mesh):
    return jax.shard_map(
        per_device,
        mesh=mesh,
        in_specs=(
            P(None, "freq", ("grp", "shot"), None),
            P(None, "freq", ("grp", "shot"), None),
            P("grp"),
        ),
        out_specs=P(None, "freq", ("grp", "shot", "sub"), None),
        check_vma=False,
    )
```

```python
import jax
import jax.numpy as jnp
from jax import lax
from jax.sharding import PartitionSpec as P

SWEEPS = 6


relaxation = 0.125
damping = 1.0


def stacked_rows(factor):
    real_left = jnp.concatenate([factor[0], factor[1]], axis=1)
    imag_left = jnp.concatenate([factor[1], -factor[0]], axis=1)
    return jnp.swapaxes(jnp.stack([real_left, imag_left], axis=1), 2, 3)


def stacked_left(factor):
    real_left = jnp.concatenate([factor[0], factor[1]], axis=1)
    imag_left = jnp.concatenate([factor[1], -factor[0]], axis=1)
    return jnp.stack([real_left, imag_left], axis=2)


def stacked_right(trace):
    return jnp.concatenate([trace[0], trace[1]], axis=1)


def sweep_whole(scaled, solution, target):
    for sweep in range(SWEEPS):
        narrow = solution.astype(jnp.bfloat16)
        real_real = jnp.einsum("qjc,qcr->qjr", narrow[0], scaled[0], preferred_element_type=jnp.float32)
        imag_imag = jnp.einsum("qjc,qcr->qjr", narrow[1], scaled[1], preferred_element_type=jnp.float32)
        real_imag = jnp.einsum("qjc,qcr->qjr", narrow[0], scaled[1], preferred_element_type=jnp.float32)
        imag_real = jnp.einsum("qjc,qcr->qjr", narrow[1], scaled[0], preferred_element_type=jnp.float32)
        image = jnp.stack([real_real - imag_imag, real_imag + imag_real])
        solution = solution + relaxation * (target - image - damping * solution)
    return solution


def strip_partials(rows, shot_count, core_count, core_index, rows_each, tile, span):
    rows = rows.astype(jnp.bfloat16)
    doubled = jnp.concatenate([rows, rows], axis=-1)
    windows = []
    for k in range(shot_count):
        start = ((k * core_count + core_index) * rows_each // tile) * tile
        windows.append(lax.dynamic_slice_in_dim(doubled[k], start, span, axis=-1))
    return jnp.stack(windows).reshape(shot_count * rows_each, *rows.shape[2:4], span)


def offset_mask(tiles, tile):
    receivers = tiles * tile
    row_tile = lax.broadcasted_iota(jnp.int32, (receivers, receivers), 0) // tile
    col_tile = lax.broadcasted_iota(jnp.int32, (receivers, receivers), 1) // tile
    return (col_tile - row_tile) % tiles <= tiles // 2


def rebuild_gram(strips, tiles, tile, direct):
    freq_local = strips.shape[1]
    receivers = tiles * tile
    span = strips.shape[-1]
    padded = jnp.pad(strips, [(0, 0)] * 3 + [(0, receivers - span)])
    padded = padded.reshape(tiles, tile, freq_local, 2, receivers)
    upper = jnp.stack([jnp.roll(padded[a], a * tile, axis=-1) for a in range(tiles)])
    upper = jnp.transpose(upper, (3, 2, 0, 1, 4)).reshape(2, freq_local, receivers, receivers)
    mirror = jnp.swapaxes(upper, 2, 3)
    mirror = jnp.stack([mirror[0], -mirror[1]])
    return jnp.where(direct, upper, mirror)


def per_device(downgoing, upgoing, source_order):
    shot_count = lax.axis_size("shot")
    core_count = lax.axis_size("sub")
    core_index = lax.axis_index("sub")
    receivers = downgoing.shape[3]
    freq_local = downgoing.shape[1]
    sources = source_order.shape[0]
    groups = shot_count * core_count
    source_local = sources // groups
    rows_each = receivers // groups
    tiles = 8 if groups % 8 == 0 else groups
    tile = receivers // tiles
    span = (tiles // 2 + 1) * tile

    right = stacked_right(downgoing)

    left = stacked_rows(downgoing).reshape(freq_local, 2, shot_count, core_count, rows_each, -1)
    left = lax.dynamic_slice_in_dim(left, core_index, 1, 3)[:, :, :, 0]
    gram_rows = jnp.einsum("qpkit,qto->kiqpo", left, right, preferred_element_type=jnp.float32)
    gram_part = strip_partials(gram_rows, shot_count, core_count, core_index, rows_each, tile, span)
    gram_strip = lax.psum_scatter(gram_part, "shot", scatter_dimension=0, tiled=True)

    local_power = jnp.sum(jnp.square(downgoing.astype(jnp.float32)), axis=(0, 2, 3))
    power = lax.psum(local_power, "shot") / receivers

    corr_all = jnp.einsum(
        "qtpu,qto->uqpo", stacked_left(upgoing), right, preferred_element_type=jnp.float32
    )
    order_table = source_order.reshape(shot_count, core_count, source_local)
    own_order = lax.dynamic_slice_in_dim(order_table, core_index, 1, 1).reshape(-1)
    corr_part = jnp.take(corr_all, own_order, axis=0).astype(jnp.bfloat16)

    direct = offset_mask(tiles, tile)
    gram_strip, power, corr_part, direct = lax.optimization_barrier((gram_strip, power, corr_part, direct))
    power_wide = power[None, :, None, None]

    shot_index = lax.axis_index("shot")
    corr_blocks = corr_part.reshape(shot_count, source_local, *corr_part.shape[1:])
    corr = lax.dynamic_index_in_dim(corr_blocks, shot_index, 0, keepdims=False).astype(jnp.float32)
    for shift in range(1, shot_count):
        outgoing = lax.dynamic_index_in_dim(corr_blocks, (shot_index + shift) % shot_count, 0, keepdims=False)
        pairs = [(k, (k + shift) % shot_count) for k in range(shot_count)]
        corr = corr + lax.ppermute(outgoing, "shot", perm=pairs).astype(jnp.float32)

    across = lax.all_gather(gram_strip, "shot", axis=0, tiled=True)
    across = across.reshape(shot_count, rows_each, freq_local, 2, span)
    across, corr = lax.optimization_barrier((across, corr))

    if core_count == 2:
        other = lax.ppermute(across, "sub", perm=[(0, 1), (1, 0)])
        first = jnp.where(core_index == 0, across, other)
        second = jnp.where(core_index == 0, other, across)
        strips = jnp.stack([first, second], axis=1)
    else:
        strips = lax.all_gather(across, "sub", axis=1, tiled=False)
    strips = strips.reshape(receivers, freq_local, 2, span)
    whole = rebuild_gram(strips, tiles, tile, direct)

    target = jnp.transpose(corr, (2, 1, 0, 3)) / power_wide

    scaled = (whole.astype(jnp.float32) / power_wide).astype(jnp.bfloat16)
    solution = jnp.zeros((2, freq_local, source_local, receivers), jnp.float32)
    return sweep_whole(scaled, solution, target)


def solution(mesh):
    return jax.shard_map(
        per_device,
        mesh=mesh,
        in_specs=(
            P(None, "freq", ("grp", "shot"), None),
            P(None, "freq", ("grp", "shot"), None),
            P("grp"),
        ),
        out_specs=P(None, "freq", ("grp", "shot", "sub"), None),
        check_vma=False,
    )
```

```python
import jax
import jax.numpy as jnp
from jax import lax
from jax.sharding import PartitionSpec as P

SWEEPS = 6


relaxation = 0.125
damping = 1.0


def stacked_rows(factor):
    real_left = jnp.concatenate([factor[0], factor[1]], axis=1)
    imag_left = jnp.concatenate([factor[1], -factor[0]], axis=1)
    return jnp.swapaxes(jnp.stack([real_left, imag_left], axis=1), 2, 3)


def stacked_left(factor):
    real_left = jnp.concatenate([factor[0], factor[1]], axis=1)
    imag_left = jnp.concatenate([factor[1], -factor[0]], axis=1)
    return jnp.stack([real_left, imag_left], axis=2)


def stacked_right(trace):
    parts, freq_local, shots, width = trace.shape
    return jnp.swapaxes(trace, 0, 1).reshape(freq_local, parts * shots, width)


def sweep_whole(scaled, solution, target):
    for sweep in range(SWEEPS):
        narrow = solution.astype(jnp.bfloat16)
        real_real = jnp.einsum("qjc,qcr->qjr", narrow[0], scaled[0], preferred_element_type=jnp.float32)
        imag_imag = jnp.einsum("qjc,qcr->qjr", narrow[1], scaled[1], preferred_element_type=jnp.float32)
        real_imag = jnp.einsum("qjc,qcr->qjr", narrow[0], scaled[1], preferred_element_type=jnp.float32)
        imag_real = jnp.einsum("qjc,qcr->qjr", narrow[1], scaled[0], preferred_element_type=jnp.float32)
        image = jnp.stack([real_real - imag_imag, real_imag + imag_real])
        solution = solution + relaxation * (target - image - damping * solution)
    return solution


def strip_partials(rows, shot_count, core_count, rows_each, tile, span):
    receivers = rows.shape[-1]
    windows = []
    for k in range(shot_count):
        start = (k * core_count * rows_each // tile) * tile
        if start + span <= receivers:
            window = rows[k, ..., start : start + span]
        else:
            window = jnp.concatenate([rows[k, ..., start:], rows[k, ..., : start + span - receivers]], axis=-1)
        windows.append(window)
    return jnp.stack(windows).astype(jnp.bfloat16).reshape(shot_count * rows_each, *rows.shape[2:4], span)


def rebuild_gram(strips, tiles, tile):
    freq_local = strips.shape[1]
    receivers = tiles * tile
    span = strips.shape[-1]
    padded = jnp.pad(strips, [(0, 0)] * 3 + [(0, receivers - span)])
    padded = padded.reshape(tiles, tile, freq_local, 2, receivers)
    upper = jnp.stack([jnp.roll(padded[a], a * tile, axis=-1) for a in range(tiles)])
    upper = jnp.transpose(upper, (3, 2, 0, 1, 4)).reshape(2, freq_local, receivers, receivers)
    mirror = jnp.swapaxes(upper, 2, 3)
    mirror = jnp.stack([mirror[0], -mirror[1]])
    row_tile = lax.broadcasted_iota(jnp.int32, (receivers, receivers), 0) // tile
    col_tile = lax.broadcasted_iota(jnp.int32, (receivers, receivers), 1) // tile
    direct = (col_tile - row_tile) % tiles <= tiles // 2
    return jnp.where(direct, upper, mirror)


def per_device(downgoing, upgoing, source_order):
    shot_count = lax.axis_size("shot")
    core_count = lax.axis_size("sub")
    core_index = lax.axis_index("sub")
    receivers = downgoing.shape[3]
    freq_local = downgoing.shape[1]
    sources = source_order.shape[0]
    groups = shot_count * core_count
    source_local = sources // groups
    rows_each = receivers // groups
    tiles = 8 if groups % 8 == 0 else groups
    tile = receivers // tiles
    span = (tiles // 2 + 1) * tile

    right = stacked_right(downgoing)

    left = stacked_rows(downgoing).reshape(freq_local, 2, shot_count, core_count, rows_each, -1)
    left = lax.dynamic_slice_in_dim(left, core_index, 1, 3)[:, :, :, 0]
    shift = (core_index * rows_each // tile) * tile
    rolled = lax.dynamic_slice_in_dim(jnp.concatenate([right, right], axis=-1), shift, receivers, axis=-1)
    gram_rows = jnp.einsum("qpkit,qto->kiqpo", left, rolled, preferred_element_type=jnp.float32)
    gram_part = strip_partials(gram_rows, shot_count, core_count, rows_each, tile, span)
    gram_strip = lax.psum_scatter(gram_part, "shot", scatter_dimension=0, tiled=True)

    local_power = jnp.sum(jnp.square(downgoing.astype(jnp.float32)), axis=(0, 2, 3))
    power = lax.psum(local_power, "shot") / receivers

    corr_all = jnp.einsum(
        "qtpu,qto->uqpo", stacked_left(upgoing), right, preferred_element_type=jnp.float32
    )
    order_table = source_order.reshape(shot_count, core_count, source_local)
    own_order = lax.dynamic_slice_in_dim(order_table, core_index, 1, 1).reshape(-1)
    corr_part = jnp.take(corr_all, own_order, axis=0).astype(jnp.bfloat16)

    gram_strip, power, corr_part = lax.optimization_barrier((gram_strip, power, corr_part))
    power_wide = power[None, :, None, None]

    shot_index = lax.axis_index("shot")
    corr_blocks = corr_part.reshape(shot_count, source_local, *corr_part.shape[1:])
    corr = lax.dynamic_index_in_dim(corr_blocks, shot_index, 0, keepdims=False).astype(jnp.float32)
    for shift in range(1, shot_count):
        outgoing = lax.dynamic_index_in_dim(corr_blocks, (shot_index + shift) % shot_count, 0, keepdims=False)
        pairs = [(k, (k + shift) % shot_count) for k in range(shot_count)]
        corr = corr + lax.ppermute(outgoing, "shot", perm=pairs).astype(jnp.float32)

    across = lax.all_gather(gram_strip, "shot", axis=0, tiled=True)
    across = across.reshape(shot_count, rows_each, freq_local, 2, span)

    if core_count == 2:
        other = lax.ppermute(across, "sub", perm=[(0, 1), (1, 0)])
        first = jnp.where(core_index == 0, across, other)
        second = jnp.where(core_index == 0, other, across)
        strips = jnp.stack([first, second], axis=1)
    else:
        strips = lax.all_gather(across, "sub", axis=1, tiled=False)
    strips = strips.reshape(receivers, freq_local, 2, span)
    whole = rebuild_gram(strips, tiles, tile)

    target = jnp.transpose(corr, (2, 1, 0, 3)) / power_wide

    scaled = (whole.astype(jnp.float32) / power_wide).astype(jnp.bfloat16)
    solution = jnp.zeros((2, freq_local, source_local, receivers), jnp.float32)
    return sweep_whole(scaled, solution, target)


def solution(mesh):
    return jax.shard_map(
        per_device,
        mesh=mesh,
        in_specs=(
            P(None, "freq", ("grp", "shot"), None),
            P(None, "freq", ("grp", "shot"), None),
            P("grp"),
        ),
        out_specs=P(None, "freq", ("grp", "shot", "sub"), None),
        check_vma=False,
    )
```

```python
import jax
import jax.numpy as jnp
from jax import lax
from jax.sharding import PartitionSpec as P

SWEEPS = 6


relaxation = 0.125
damping = 1.0


def stacked_rows(factor):
    real_left = jnp.concatenate([factor[0], factor[1]], axis=1)
    imag_left = jnp.concatenate([factor[1], -factor[0]], axis=1)
    return jnp.swapaxes(jnp.stack([real_left, imag_left], axis=1), 2, 3)


def stacked_left(factor):
    real_left = jnp.concatenate([factor[0], factor[1]], axis=1)
    imag_left = jnp.concatenate([factor[1], -factor[0]], axis=1)
    return jnp.stack([real_left, imag_left], axis=2)


def stacked_right(trace):
    return jnp.concatenate([trace[0], trace[1]], axis=1)


def sweep_whole(scaled, solution, target):
    for sweep in range(SWEEPS):
        narrow = solution.astype(jnp.bfloat16)
        real_real = jnp.einsum("qjc,qcr->qjr", narrow[0], scaled[0], preferred_element_type=jnp.float32)
        imag_imag = jnp.einsum("qjc,qcr->qjr", narrow[1], scaled[1], preferred_element_type=jnp.float32)
        real_imag = jnp.einsum("qjc,qcr->qjr", narrow[0], scaled[1], preferred_element_type=jnp.float32)
        imag_real = jnp.einsum("qjc,qcr->qjr", narrow[1], scaled[0], preferred_element_type=jnp.float32)
        image = jnp.stack([real_real - imag_imag, real_imag + imag_real])
        solution = solution + relaxation * (target - image - damping * solution)
    return solution


def strip_partials(rows, shot_count, core_count, core_index, rows_each, tile, span):
    rows = rows.astype(jnp.bfloat16)
    doubled = jnp.concatenate([rows, rows], axis=-1)
    windows = []
    for k in range(shot_count):
        start = ((k * core_count + core_index) * rows_each // tile) * tile
        windows.append(lax.dynamic_slice_in_dim(doubled[k], start, span, axis=-1))
    return jnp.stack(windows).reshape(shot_count * rows_each, *rows.shape[2:4], span)


def rebuild_gram(strips, tiles, tile):
    freq_local = strips.shape[1]
    receivers = tiles * tile
    span = strips.shape[-1]
    padded = jnp.pad(strips, [(0, 0)] * 3 + [(0, receivers - span)])
    padded = padded.reshape(tiles, tile, freq_local, 2, receivers)
    upper = jnp.stack([jnp.roll(padded[a], a * tile, axis=-1) for a in range(tiles)])
    upper = jnp.transpose(upper, (3, 2, 0, 1, 4)).reshape(2, freq_local, receivers, receivers)
    mirror = jnp.swapaxes(upper, 2, 3)
    mirror = jnp.stack([mirror[0], -mirror[1]])
    row_tile = lax.broadcasted_iota(jnp.int32, (receivers, receivers), 0) // tile
    col_tile = lax.broadcasted_iota(jnp.int32, (receivers, receivers), 1) // tile
    direct = (col_tile - row_tile) % tiles <= tiles // 2
    return jnp.where(direct, upper, mirror)


def exchange_sum(partials, shot_count, shot_index):
    blocks = partials.reshape(shot_count, partials.shape[0] // shot_count, *partials.shape[1:])
    total = lax.dynamic_index_in_dim(blocks, shot_index, 0, keepdims=False).astype(jnp.float32)
    for shift in range(1, shot_count):
        outgoing = lax.dynamic_index_in_dim(blocks, (shot_index + shift) % shot_count, 0, keepdims=False)
        pairs = [(k, (k + shift) % shot_count) for k in range(shot_count)]
        total = total + lax.ppermute(outgoing, "shot", perm=pairs).astype(jnp.float32)
    return total


def per_device(downgoing, upgoing, source_order):
    shot_count = lax.axis_size("shot")
    core_count = lax.axis_size("sub")
    core_index = lax.axis_index("sub")
    receivers = downgoing.shape[3]
    freq_local = downgoing.shape[1]
    sources = source_order.shape[0]
    groups = shot_count * core_count
    source_local = sources // groups
    rows_each = receivers // groups
    tiles = 8 if groups % 8 == 0 else groups
    tile = receivers // tiles
    span = (tiles // 2 + 1) * tile

    right = stacked_right(downgoing)

    left = stacked_rows(downgoing).reshape(freq_local, 2, shot_count, core_count, rows_each, -1)
    left = lax.dynamic_slice_in_dim(left, core_index, 1, 3)[:, :, :, 0]
    gram_rows = jnp.einsum("qpkit,qto->kiqpo", left, right, preferred_element_type=jnp.float32)
    gram_part = strip_partials(gram_rows, shot_count, core_count, core_index, rows_each, tile, span)
    shot_index = lax.axis_index("shot")
    gram_strip = exchange_sum(gram_part, shot_count, shot_index).astype(jnp.bfloat16)

    local_power = jnp.sum(jnp.square(downgoing.astype(jnp.float32)), axis=(0, 2, 3))
    power = lax.psum(local_power, "shot") / receivers

    corr_all = jnp.einsum(
        "qtpu,qto->uqpo", stacked_left(upgoing), right, preferred_element_type=jnp.float32
    )
    order_table = source_order.reshape(shot_count, core_count, source_local)
    own_order = lax.dynamic_slice_in_dim(order_table, core_index, 1, 1).reshape(-1)
    corr_part = jnp.take(corr_all, own_order, axis=0).astype(jnp.bfloat16)

    gram_strip, power, corr_part = lax.optimization_barrier((gram_strip, power, corr_part))
    power_wide = power[None, :, None, None]

    corr = exchange_sum(corr_part, shot_count, shot_index)

    across = lax.all_gather(gram_strip, "shot", axis=0, tiled=True)
    across = across.reshape(shot_count, rows_each, freq_local, 2, span)

    if core_count == 2:
        other = lax.ppermute(across, "sub", perm=[(0, 1), (1, 0)])
        first = jnp.where(core_index == 0, across, other)
        second = jnp.where(core_index == 0, other, across)
        strips = jnp.stack([first, second], axis=1)
    else:
        strips = lax.all_gather(across, "sub", axis=1, tiled=False)
    strips = strips.reshape(receivers, freq_local, 2, span)
    whole = rebuild_gram(strips, tiles, tile)

    target = jnp.transpose(corr, (2, 1, 0, 3)) / power_wide

    scaled = (whole.astype(jnp.float32) / power_wide).astype(jnp.bfloat16)
    solution = jnp.zeros((2, freq_local, source_local, receivers), jnp.float32)
    return sweep_whole(scaled, solution, target)


def solution(mesh):
    return jax.shard_map(
        per_device,
        mesh=mesh,
        in_specs=(
            P(None, "freq", ("grp", "shot"), None),
            P(None, "freq", ("grp", "shot"), None),
            P("grp"),
        ),
        out_specs=P(None, "freq", ("grp", "shot", "sub"), None),
        check_vma=False,
    )
```

```python
import jax
import jax.numpy as jnp
from jax import lax
from jax.sharding import PartitionSpec as P

SWEEPS = 6


relaxation = 0.125
damping = 1.0


def stacked_rows(factor):
    real_left = jnp.concatenate([factor[0], factor[1]], axis=1)
    imag_left = jnp.concatenate([factor[1], -factor[0]], axis=1)
    return jnp.swapaxes(jnp.stack([real_left, imag_left], axis=1), 2, 3)


def stacked_left(factor):
    real_left = jnp.concatenate([factor[0], factor[1]], axis=1)
    imag_left = jnp.concatenate([factor[1], -factor[0]], axis=1)
    return jnp.stack([real_left, imag_left], axis=2)


def stacked_right(trace):
    return jnp.concatenate([trace[0], trace[1]], axis=1)


def sweep_whole(scaled, solution, target):
    for sweep in range(SWEEPS):
        narrow = solution.astype(jnp.bfloat16)
        real_real = jnp.einsum("qjc,qcr->qjr", narrow[0], scaled[0], preferred_element_type=jnp.float32)
        imag_imag = jnp.einsum("qjc,qcr->qjr", narrow[1], scaled[1], preferred_element_type=jnp.float32)
        real_imag = jnp.einsum("qjc,qcr->qjr", narrow[0], scaled[1], preferred_element_type=jnp.float32)
        imag_real = jnp.einsum("qjc,qcr->qjr", narrow[1], scaled[0], preferred_element_type=jnp.float32)
        image = jnp.stack([real_real - imag_imag, real_imag + imag_real])
        solution = solution + relaxation * (target - image - damping * solution)
    return solution


def strip_partials(rows, shot_count, core_count, core_index, rows_each, tile, span):
    rows = rows.astype(jnp.bfloat16)
    doubled = jnp.concatenate([rows, rows], axis=-1)
    windows = []
    for k in range(shot_count):
        start = ((k * core_count + core_index) * rows_each // tile) * tile
        windows.append(lax.dynamic_slice_in_dim(doubled[k], start, span, axis=-1))
    return jnp.stack(windows).reshape(shot_count * rows_each, *rows.shape[2:4], span)


def rebuild_gram(strips, tiles, tile):
    freq_local = strips.shape[1]
    receivers = tiles * tile
    span = strips.shape[-1]
    padded = jnp.pad(strips, [(0, 0)] * 3 + [(0, receivers - span)])
    padded = padded.reshape(tiles, tile, freq_local, 2, receivers)
    upper = jnp.stack([jnp.roll(padded[a], a * tile, axis=-1) for a in range(tiles)])
    upper = jnp.transpose(upper, (3, 2, 0, 1, 4)).reshape(2, freq_local, receivers, receivers)
    mirror = jnp.swapaxes(upper, 2, 3)
    mirror = jnp.stack([mirror[0], -mirror[1]])
    row_tile = lax.broadcasted_iota(jnp.int32, (tiles, 1, tiles, 1), 0)
    col_tile = lax.broadcasted_iota(jnp.int32, (tiles, 1, tiles, 1), 2)
    direct = (col_tile - row_tile) % tiles <= tiles // 2
    shape6 = (2, freq_local, tiles, tile, tiles, tile)
    whole = jnp.where(direct, upper.reshape(shape6), mirror.reshape(shape6))
    return whole.reshape(upper.shape)


def per_device(downgoing, upgoing, source_order):
    shot_count = lax.axis_size("shot")
    core_count = lax.axis_size("sub")
    core_index = lax.axis_index("sub")
    receivers = downgoing.shape[3]
    freq_local = downgoing.shape[1]
    sources = source_order.shape[0]
    groups = shot_count * core_count
    source_local = sources // groups
    rows_each = receivers // groups
    tiles = 8 if groups % 8 == 0 else groups
    tile = receivers // tiles
    span = (tiles // 2 + 1) * tile

    right = stacked_right(downgoing)

    left = stacked_rows(downgoing).reshape(freq_local, 2, shot_count, core_count, rows_each, -1)
    left = lax.dynamic_slice_in_dim(left, core_index, 1, 3)[:, :, :, 0]
    gram_rows = jnp.einsum("qpkit,qto->kiqpo", left, right, preferred_element_type=jnp.float32)
    gram_part = strip_partials(gram_rows, shot_count, core_count, core_index, rows_each, tile, span)
    gram_strip = lax.psum_scatter(gram_part, "shot", scatter_dimension=0, tiled=True)

    local_power = jnp.sum(jnp.square(downgoing.astype(jnp.float32)), axis=(0, 2, 3))
    power = lax.psum(local_power, "shot") / receivers

    corr_all = jnp.einsum(
        "qtpu,qto->uqpo", stacked_left(upgoing), right, preferred_element_type=jnp.float32
    )
    order_table = source_order.reshape(shot_count, core_count, source_local)
    own_order = lax.dynamic_slice_in_dim(order_table, core_index, 1, 1).reshape(-1)
    corr_part = jnp.take(corr_all, own_order, axis=0).astype(jnp.bfloat16)

    gram_strip, power, corr_part = lax.optimization_barrier((gram_strip, power, corr_part))
    power_wide = power[None, :, None, None]

    shot_index = lax.axis_index("shot")
    corr_blocks = corr_part.reshape(shot_count, source_local, *corr_part.shape[1:])
    corr = lax.dynamic_index_in_dim(corr_blocks, shot_index, 0, keepdims=False).astype(jnp.float32)
    for shift in range(1, shot_count):
        outgoing = lax.dynamic_index_in_dim(corr_blocks, (shot_index + shift) % shot_count, 0, keepdims=False)
        pairs = [(k, (k + shift) % shot_count) for k in range(shot_count)]
        corr = corr + lax.ppermute(outgoing, "shot", perm=pairs).astype(jnp.float32)

    across = lax.all_gather(gram_strip, "shot", axis=0, tiled=True)
    across = across.reshape(shot_count, rows_each, freq_local, 2, span)

    if core_count == 2:
        other = lax.ppermute(across, "sub", perm=[(0, 1), (1, 0)])
        first = jnp.where(core_index == 0, across, other)
        second = jnp.where(core_index == 0, other, across)
        strips = jnp.stack([first, second], axis=1)
    else:
        strips = lax.all_gather(across, "sub", axis=1, tiled=False)
    strips = strips.reshape(receivers, freq_local, 2, span)
    whole = rebuild_gram(strips, tiles, tile)

    target = jnp.transpose(corr, (2, 1, 0, 3)) / power_wide

    scaled = (whole.astype(jnp.float32) / power_wide).astype(jnp.bfloat16)
    solution = jnp.zeros((2, freq_local, source_local, receivers), jnp.float32)
    return sweep_whole(scaled, solution, target)


def solution(mesh):
    return jax.shard_map(
        per_device,
        mesh=mesh,
        in_specs=(
            P(None, "freq", ("grp", "shot"), None),
            P(None, "freq", ("grp", "shot"), None),
            P("grp"),
        ),
        out_specs=P(None, "freq", ("grp", "shot", "sub"), None),
        check_vma=False,
    )
```

```python
import jax
import jax.numpy as jnp
from jax import lax
from jax.sharding import PartitionSpec as P

SWEEPS = 6


relaxation = 0.125
damping = 1.0


def stacked_rows(factor):
    real_left = jnp.concatenate([factor[0], factor[1]], axis=1)
    imag_left = jnp.concatenate([factor[1], -factor[0]], axis=1)
    return jnp.swapaxes(jnp.stack([real_left, imag_left], axis=1), 2, 3)


def stacked_left(factor):
    real_left = jnp.concatenate([factor[0], factor[1]], axis=1)
    imag_left = jnp.concatenate([factor[1], -factor[0]], axis=1)
    return jnp.stack([real_left, imag_left], axis=2)


def stacked_right(trace):
    return jnp.concatenate([trace[0], trace[1]], axis=1)


def sweep_whole(scaled, solution, target):
    solution = solution + relaxation * (target - damping * solution)
    for sweep in range(1, SWEEPS):
        narrow = solution.astype(jnp.bfloat16)
        real_real = jnp.einsum("qjc,qcr->qjr", narrow[0], scaled[0], preferred_element_type=jnp.float32)
        imag_imag = jnp.einsum("qjc,qcr->qjr", narrow[1], scaled[1], preferred_element_type=jnp.float32)
        real_imag = jnp.einsum("qjc,qcr->qjr", narrow[0], scaled[1], preferred_element_type=jnp.float32)
        imag_real = jnp.einsum("qjc,qcr->qjr", narrow[1], scaled[0], preferred_element_type=jnp.float32)
        image = jnp.stack([real_real - imag_imag, real_imag + imag_real])
        solution = solution + relaxation * (target - image - damping * solution)
    return solution


def strip_partials(rows, shot_count, core_count, core_index, rows_each, tile, span):
    rows = rows.astype(jnp.bfloat16)
    doubled = jnp.concatenate([rows, rows], axis=-1)
    windows = []
    for k in range(shot_count):
        start = ((k * core_count + core_index) * rows_each // tile) * tile
        windows.append(lax.dynamic_slice_in_dim(doubled[k], start, span, axis=-1))
    return jnp.stack(windows).reshape(shot_count * rows_each, *rows.shape[2:4], span)


def rebuild_gram(strips, tiles, tile):
    freq_local = strips.shape[1]
    receivers = tiles * tile
    span = strips.shape[-1]
    padded = jnp.pad(strips, [(0, 0)] * 3 + [(0, receivers - span)])
    padded = padded.reshape(tiles, tile, freq_local, 2, receivers)
    upper = jnp.stack([jnp.roll(padded[a], a * tile, axis=-1) for a in range(tiles)])
    upper = jnp.transpose(upper, (3, 2, 0, 1, 4)).reshape(2, freq_local, receivers, receivers)
    mirror = jnp.swapaxes(upper, 2, 3)
    mirror = jnp.stack([mirror[0], -mirror[1]])
    row_tile = lax.broadcasted_iota(jnp.int32, (tiles, 1, tiles, 1), 0)
    col_tile = lax.broadcasted_iota(jnp.int32, (tiles, 1, tiles, 1), 2)
    direct = (col_tile - row_tile) % tiles <= tiles // 2
    shape6 = (2, freq_local, tiles, tile, tiles, tile)
    whole = jnp.where(direct, upper.reshape(shape6), mirror.reshape(shape6))
    return whole.reshape(upper.shape)


def per_device(downgoing, upgoing, source_order):
    shot_count = lax.axis_size("shot")
    core_count = lax.axis_size("sub")
    core_index = lax.axis_index("sub")
    receivers = downgoing.shape[3]
    freq_local = downgoing.shape[1]
    sources = source_order.shape[0]
    groups = shot_count * core_count
    source_local = sources // groups
    rows_each = receivers // groups
    tiles = 8 if groups % 8 == 0 else groups
    tile = receivers // tiles
    span = (tiles // 2 + 1) * tile

    right = stacked_right(downgoing)

    left = stacked_rows(downgoing).reshape(freq_local, 2, shot_count, core_count, rows_each, -1)
    left = lax.dynamic_slice_in_dim(left, core_index, 1, 3)[:, :, :, 0]
    gram_rows = jnp.einsum("qpkit,qto->kiqpo", left, right, preferred_element_type=jnp.float32)
    gram_part = strip_partials(gram_rows, shot_count, core_count, core_index, rows_each, tile, span)
    gram_strip = lax.psum_scatter(gram_part, "shot", scatter_dimension=0, tiled=True)

    local_power = jnp.sum(jnp.square(downgoing.astype(jnp.float32)), axis=(0, 2, 3))
    power = lax.psum(local_power, "shot") / receivers

    corr_all = jnp.einsum(
        "qtpu,qto->uqpo", stacked_left(upgoing), right, preferred_element_type=jnp.float32
    )
    order_table = source_order.reshape(shot_count, core_count, source_local)
    own_order = lax.dynamic_slice_in_dim(order_table, core_index, 1, 1).reshape(-1)
    corr_part = jnp.take(corr_all, own_order, axis=0).astype(jnp.bfloat16)

    gram_strip, power, corr_part = lax.optimization_barrier((gram_strip, power, corr_part))
    power_wide = power[None, :, None, None]

    shot_index = lax.axis_index("shot")
    corr_blocks = corr_part.reshape(shot_count, source_local, *corr_part.shape[1:])
    corr = lax.dynamic_index_in_dim(corr_blocks, shot_index, 0, keepdims=False).astype(jnp.float32)
    for shift in range(1, shot_count):
        outgoing = lax.dynamic_index_in_dim(corr_blocks, (shot_index + shift) % shot_count, 0, keepdims=False)
        pairs = [(k, (k + shift) % shot_count) for k in range(shot_count)]
        corr = corr + lax.ppermute(outgoing, "shot", perm=pairs).astype(jnp.float32)

    across = lax.all_gather(gram_strip, "shot", axis=0, tiled=True)
    across = across.reshape(shot_count, rows_each, freq_local, 2, span)

    if core_count == 2:
        other = lax.ppermute(across, "sub", perm=[(0, 1), (1, 0)])
        first = jnp.where(core_index == 0, across, other)
        second = jnp.where(core_index == 0, other, across)
        strips = jnp.stack([first, second], axis=1)
    else:
        strips = lax.all_gather(across, "sub", axis=1, tiled=False)
    strips = strips.reshape(receivers, freq_local, 2, span)
    whole = rebuild_gram(strips, tiles, tile)

    target = jnp.transpose(corr, (2, 1, 0, 3)) / power_wide

    scaled = (whole.astype(jnp.float32) / power_wide).astype(jnp.bfloat16)
    solution = jnp.zeros((2, freq_local, source_local, receivers), jnp.float32)
    return sweep_whole(scaled, solution, target)


def solution(mesh):
    return jax.shard_map(
        per_device,
        mesh=mesh,
        in_specs=(
            P(None, "freq", ("grp", "shot"), None),
            P(None, "freq", ("grp", "shot"), None),
            P("grp"),
        ),
        out_specs=P(None, "freq", ("grp", "shot", "sub"), None),
        check_vma=False,
    )
```

```python
import jax
import jax.numpy as jnp
from jax import lax
from jax.sharding import PartitionSpec as P

SWEEPS = 6


relaxation = 0.125
damping = 1.0


def stacked_rows(factor):
    real_left = jnp.concatenate([factor[0], factor[1]], axis=1)
    imag_left = jnp.concatenate([factor[1], -factor[0]], axis=1)
    return jnp.swapaxes(jnp.stack([real_left, imag_left], axis=1), 2, 3)


def stacked_left(factor):
    real_left = jnp.concatenate([factor[0], factor[1]], axis=1)
    imag_left = jnp.concatenate([factor[1], -factor[0]], axis=1)
    return jnp.stack([real_left, imag_left], axis=2)


def stacked_right(trace):
    return jnp.concatenate([trace[0], trace[1]], axis=1)


def sweep_whole(scaled, solution, target):
    for sweep in range(SWEEPS):
        narrow = solution.astype(jnp.bfloat16)
        real_real = jnp.einsum("qjc,qcr->qjr", narrow[0], scaled[0], preferred_element_type=jnp.float32)
        imag_imag = jnp.einsum("qjc,qcr->qjr", narrow[1], scaled[1], preferred_element_type=jnp.float32)
        real_imag = jnp.einsum("qjc,qcr->qjr", narrow[0], scaled[1], preferred_element_type=jnp.float32)
        imag_real = jnp.einsum("qjc,qcr->qjr", narrow[1], scaled[0], preferred_element_type=jnp.float32)
        image = jnp.stack([real_real - imag_imag, real_imag + imag_real])
        solution = solution + relaxation * (target - image - damping * solution)
    return solution


def strip_partials(rows, shot_count, core_count, core_index, rows_each, tile, span):
    rows = rows.astype(jnp.bfloat16)
    doubled = jnp.concatenate([rows, rows], axis=-1)
    windows = []
    for k in range(shot_count):
        start = ((k * core_count + core_index) * rows_each // tile) * tile
        windows.append(lax.dynamic_slice_in_dim(doubled[k], start, span, axis=-1))
    return jnp.stack(windows).reshape(shot_count * rows_each, *rows.shape[2:4], span)


def rebuild_gram(strips, tiles, tile):
    freq_local = strips.shape[1]
    receivers = tiles * tile
    span = strips.shape[-1]
    padded = jnp.pad(strips, [(0, 0)] * 3 + [(0, receivers - span)])
    padded = padded.reshape(tiles, tile, freq_local, 2, receivers)
    upper = jnp.stack([jnp.roll(padded[a], a * tile, axis=-1) for a in range(tiles)])
    upper = jnp.transpose(upper, (3, 2, 0, 1, 4)).reshape(2, freq_local, receivers, receivers)
    mirror = jnp.swapaxes(upper, 2, 3)
    mirror = jnp.stack([mirror[0], -mirror[1]])
    row_tile = lax.broadcasted_iota(jnp.int32, (tiles, 1, tiles, 1), 0)
    col_tile = lax.broadcasted_iota(jnp.int32, (tiles, 1, tiles, 1), 2)
    direct = (col_tile - row_tile) % tiles <= tiles // 2
    shape6 = (2, freq_local, tiles, tile, tiles, tile)
    whole = jnp.where(direct, upper.reshape(shape6), mirror.reshape(shape6))
    return whole.reshape(upper.shape)


def line_gather(block, shot_count, shot_index):
    rightward = [(k, k + 1) for k in range(shot_count - 1)]
    leftward = [(k + 1, k) for k in range(shot_count - 1)]
    from_below, from_above = [], []
    moving_up, moving_down = block, block
    for step in range(1, shot_count):
        moving_up = lax.ppermute(moving_up, "shot", perm=rightward)
        moving_down = lax.ppermute(moving_down, "shot", perm=leftward)
        from_below.append(moving_up)
        from_above.append(moving_down)
    arrivals = jnp.stack(from_below[::-1] + [block] + from_above)
    return jnp.stack(
        [
            lax.dynamic_index_in_dim(arrivals, k + shot_count - 1 - shot_index, 0, keepdims=False)
            for k in range(shot_count)
        ]
    )


def per_device(downgoing, upgoing, source_order):
    shot_count = lax.axis_size("shot")
    core_count = lax.axis_size("sub")
    core_index = lax.axis_index("sub")
    receivers = downgoing.shape[3]
    freq_local = downgoing.shape[1]
    sources = source_order.shape[0]
    groups = shot_count * core_count
    source_local = sources // groups
    rows_each = receivers // groups
    tiles = 8 if groups % 8 == 0 else groups
    tile = receivers // tiles
    span = (tiles // 2 + 1) * tile

    right = stacked_right(downgoing)

    left = stacked_rows(downgoing).reshape(freq_local, 2, shot_count, core_count, rows_each, -1)
    left = lax.dynamic_slice_in_dim(left, core_index, 1, 3)[:, :, :, 0]
    gram_rows = jnp.einsum("qpkit,qto->kiqpo", left, right, preferred_element_type=jnp.float32)
    gram_part = strip_partials(gram_rows, shot_count, core_count, core_index, rows_each, tile, span)
    gram_strip = lax.psum_scatter(gram_part, "shot", scatter_dimension=0, tiled=True)

    local_power = jnp.sum(jnp.square(downgoing.astype(jnp.float32)), axis=(0, 2, 3))
    power = lax.psum(local_power, "shot") / receivers

    corr_all = jnp.einsum(
        "qtpu,qto->uqpo", stacked_left(upgoing), right, preferred_element_type=jnp.float32
    )
    order_table = source_order.reshape(shot_count, core_count, source_local)
    own_order = lax.dynamic_slice_in_dim(order_table, core_index, 1, 1).reshape(-1)
    corr_part = jnp.take(corr_all, own_order, axis=0).astype(jnp.bfloat16)

    gram_strip, power, corr_part = lax.optimization_barrier((gram_strip, power, corr_part))
    power_wide = power[None, :, None, None]

    shot_index = lax.axis_index("shot")
    corr_blocks = corr_part.reshape(shot_count, source_local, *corr_part.shape[1:])
    corr = lax.dynamic_index_in_dim(corr_blocks, shot_index, 0, keepdims=False).astype(jnp.float32)
    for shift in range(1, shot_count):
        outgoing = lax.dynamic_index_in_dim(corr_blocks, (shot_index + shift) % shot_count, 0, keepdims=False)
        pairs = [(k, (k + shift) % shot_count) for k in range(shot_count)]
        corr = corr + lax.ppermute(outgoing, "shot", perm=pairs).astype(jnp.float32)

    across = line_gather(gram_strip, shot_count, shot_index)

    if core_count == 2:
        other = lax.ppermute(across, "sub", perm=[(0, 1), (1, 0)])
        first = jnp.where(core_index == 0, across, other)
        second = jnp.where(core_index == 0, other, across)
        strips = jnp.stack([first, second], axis=1)
    else:
        strips = lax.all_gather(across, "sub", axis=1, tiled=False)
    strips = strips.reshape(receivers, freq_local, 2, span)
    whole = rebuild_gram(strips, tiles, tile)

    target = jnp.transpose(corr, (2, 1, 0, 3)) / power_wide

    scaled = (whole.astype(jnp.float32) / power_wide).astype(jnp.bfloat16)
    solution = jnp.zeros((2, freq_local, source_local, receivers), jnp.float32)
    return sweep_whole(scaled, solution, target)


def solution(mesh):
    return jax.shard_map(
        per_device,
        mesh=mesh,
        in_specs=(
            P(None, "freq", ("grp", "shot"), None),
            P(None, "freq", ("grp", "shot"), None),
            P("grp"),
        ),
        out_specs=P(None, "freq", ("grp", "shot", "sub"), None),
        check_vma=False,
    )
```

```python
import jax
import jax.numpy as jnp
from jax import lax
from jax.sharding import PartitionSpec as P

SWEEPS = 6


relaxation = 0.125
damping = 1.0


def stacked_rows(factor):
    real_left = jnp.concatenate([factor[0], factor[1]], axis=1)
    imag_left = jnp.concatenate([factor[1], -factor[0]], axis=1)
    return jnp.swapaxes(jnp.stack([real_left, imag_left], axis=1), 2, 3)


def stacked_left(factor):
    real_left = jnp.concatenate([factor[0], factor[1]], axis=1)
    imag_left = jnp.concatenate([factor[1], -factor[0]], axis=1)
    return jnp.stack([real_left, imag_left], axis=2)


def stacked_right(trace):
    return jnp.concatenate([trace[0], trace[1]], axis=1)


def sweep_whole(scaled, solution, target):
    for sweep in range(SWEEPS):
        narrow = solution.astype(jnp.bfloat16)
        real_real = jnp.einsum("qjc,qcr->qjr", narrow[0], scaled[0], preferred_element_type=jnp.float32)
        imag_imag = jnp.einsum("qjc,qcr->qjr", narrow[1], scaled[1], preferred_element_type=jnp.float32)
        real_imag = jnp.einsum("qjc,qcr->qjr", narrow[0], scaled[1], preferred_element_type=jnp.float32)
        imag_real = jnp.einsum("qjc,qcr->qjr", narrow[1], scaled[0], preferred_element_type=jnp.float32)
        image = jnp.stack([real_real - imag_imag, real_imag + imag_real])
        solution = solution + relaxation * (target - image - damping * solution)
    return solution


def strip_partials(rows, shot_count, core_count, core_index, rows_each, tile, span):
    rows = rows.astype(jnp.bfloat16)
    doubled = jnp.concatenate([rows, rows], axis=-1)
    windows = []
    for k in range(shot_count):
        start = ((k * core_count + core_index) * rows_each // tile) * tile
        windows.append(lax.dynamic_slice_in_dim(doubled[k], start, span, axis=-1))
    return jnp.stack(windows).reshape(shot_count * rows_each, *rows.shape[2:4], span)


def rebuild_gram(strips, tiles, tile):
    freq_local = strips.shape[1]
    receivers = tiles * tile
    span = strips.shape[-1]
    padded = jnp.pad(strips, [(0, 0)] * 3 + [(0, receivers - span)])
    padded = padded.reshape(tiles, tile, freq_local, 2, receivers)
    upper = jnp.stack([jnp.roll(padded[a], a * tile, axis=-1) for a in range(tiles)])
    upper = jnp.transpose(upper, (3, 2, 0, 1, 4)).reshape(2, freq_local, receivers, receivers)
    mirror = jnp.swapaxes(upper, 2, 3)
    mirror = jnp.stack([mirror[0], -mirror[1]])
    row_tile = lax.broadcasted_iota(jnp.int32, (tiles, 1, tiles, 1), 0)
    col_tile = lax.broadcasted_iota(jnp.int32, (tiles, 1, tiles, 1), 2)
    direct = (col_tile - row_tile) % tiles <= tiles // 2
    shape6 = (2, freq_local, tiles, tile, tiles, tile)
    whole = jnp.where(direct, upper.reshape(shape6), mirror.reshape(shape6))
    return whole.reshape(upper.shape)


def per_device(downgoing, upgoing, source_order):
    shot_count = lax.axis_size("shot")
    core_count = lax.axis_size("sub")
    core_index = lax.axis_index("sub")
    receivers = downgoing.shape[3]
    freq_local = downgoing.shape[1]
    sources = source_order.shape[0]
    groups = shot_count * core_count
    source_local = sources // groups
    rows_each = receivers // groups
    tiles = 8 if groups % 8 == 0 else groups
    tile = receivers // tiles
    span = (tiles // 2 + 1) * tile

    right = stacked_right(downgoing)

    left = stacked_rows(downgoing).reshape(freq_local, 2, shot_count, core_count, rows_each, -1)
    left = lax.dynamic_slice_in_dim(left, core_index, 1, 3)[:, :, :, 0]
    gram_rows = jnp.einsum("qpkit,qto->kiqpo", left, right, preferred_element_type=jnp.float32)
    gram_part = strip_partials(gram_rows, shot_count, core_count, core_index, rows_each, tile, span)
    gram_strip = lax.psum_scatter(gram_part, "shot", scatter_dimension=0, tiled=True)

    corr_all = jnp.einsum(
        "qtpu,qto->uqpo", stacked_left(upgoing), right, preferred_element_type=jnp.float32
    )
    order_table = source_order.reshape(shot_count, core_count, source_local)
    own_order = lax.dynamic_slice_in_dim(order_table, core_index, 1, 1).reshape(-1)
    corr_part = jnp.take(corr_all, own_order, axis=0).astype(jnp.bfloat16)

    gram_strip, corr_part, power_trace = lax.optimization_barrier((gram_strip, corr_part, downgoing))

    shot_index = lax.axis_index("shot")
    corr_blocks = corr_part.reshape(shot_count, source_local, *corr_part.shape[1:])
    corr = lax.dynamic_index_in_dim(corr_blocks, shot_index, 0, keepdims=False).astype(jnp.float32)
    for shift in range(1, shot_count):
        outgoing = lax.dynamic_index_in_dim(corr_blocks, (shot_index + shift) % shot_count, 0, keepdims=False)
        pairs = [(k, (k + shift) % shot_count) for k in range(shot_count)]
        corr = corr + lax.ppermute(outgoing, "shot", perm=pairs).astype(jnp.float32)

    across = lax.all_gather(gram_strip, "shot", axis=0, tiled=True)
    across = across.reshape(shot_count, rows_each, freq_local, 2, span)
    local_power = jnp.sum(jnp.square(power_trace.astype(jnp.float32)), axis=(0, 2, 3))
    power = lax.psum(local_power, "shot") / receivers
    across, power = lax.optimization_barrier((across, power))
    power_wide = power[None, :, None, None]

    if core_count == 2:
        other = lax.ppermute(across, "sub", perm=[(0, 1), (1, 0)])
        first = jnp.where(core_index == 0, across, other)
        second = jnp.where(core_index == 0, other, across)
        strips = jnp.stack([first, second], axis=1)
    else:
        strips = lax.all_gather(across, "sub", axis=1, tiled=False)
    strips = strips.reshape(receivers, freq_local, 2, span)
    whole = rebuild_gram(strips, tiles, tile)

    target = jnp.transpose(corr, (2, 1, 0, 3)) / power_wide

    scaled = (whole.astype(jnp.float32) / power_wide).astype(jnp.bfloat16)
    solution = jnp.zeros((2, freq_local, source_local, receivers), jnp.float32)
    return sweep_whole(scaled, solution, target)


def solution(mesh):
    return jax.shard_map(
        per_device,
        mesh=mesh,
        in_specs=(
            P(None, "freq", ("grp", "shot"), None),
            P(None, "freq", ("grp", "shot"), None),
            P("grp"),
        ),
        out_specs=P(None, "freq", ("grp", "shot", "sub"), None),
        check_vma=False,
    )
```

```python
import jax
import jax.numpy as jnp
from jax import lax
from jax.sharding import PartitionSpec as P

SWEEPS = 6


relaxation = 0.125
damping = 1.0


def stacked_rows(factor):
    real_left = jnp.concatenate([factor[0], factor[1]], axis=1)
    imag_left = jnp.concatenate([factor[1], -factor[0]], axis=1)
    return jnp.swapaxes(jnp.stack([real_left, imag_left], axis=1), 2, 3)


def stacked_left(factor):
    real_left = jnp.concatenate([factor[0], factor[1]], axis=1)
    imag_left = jnp.concatenate([factor[1], -factor[0]], axis=1)
    return jnp.stack([real_left, imag_left], axis=2)


def stacked_right(trace):
    return jnp.concatenate([trace[0], trace[1]], axis=1)


def sweep_whole(scaled, solution, target):
    freq_local, receivers = scaled.shape[1], scaled.shape[-1]
    sources = target.shape[2]
    wide = jnp.transpose(scaled, (1, 2, 0, 3)).reshape(freq_local, receivers, 2 * receivers)
    for sweep in range(SWEEPS):
        narrow = solution.astype(jnp.bfloat16)
        stacked = jnp.concatenate([narrow[0], narrow[1]], axis=1)
        products = jnp.einsum("qjc,qcr->qjr", stacked, wide, preferred_element_type=jnp.float32)
        real_real = products[:, :sources, :receivers]
        real_imag = products[:, :sources, receivers:]
        imag_real = products[:, sources:, :receivers]
        imag_imag = products[:, sources:, receivers:]
        image = jnp.stack([real_real - imag_imag, real_imag + imag_real])
        solution = solution + relaxation * (target - image - damping * solution)
    return solution


def strip_partials(rows, shot_count, core_count, core_index, rows_each, tile, span):
    rows = rows.astype(jnp.bfloat16)
    doubled = jnp.concatenate([rows, rows], axis=-1)
    windows = []
    for k in range(shot_count):
        start = ((k * core_count + core_index) * rows_each // tile) * tile
        windows.append(lax.dynamic_slice_in_dim(doubled[k], start, span, axis=-1))
    return jnp.stack(windows).reshape(shot_count * rows_each, *rows.shape[2:4], span)


def rebuild_gram(strips, tiles, tile):
    freq_local = strips.shape[1]
    receivers = tiles * tile
    span = strips.shape[-1]
    padded = jnp.pad(strips, [(0, 0)] * 3 + [(0, receivers - span)])
    padded = padded.reshape(tiles, tile, freq_local, 2, receivers)
    upper = jnp.stack([jnp.roll(padded[a], a * tile, axis=-1) for a in range(tiles)])
    upper = jnp.transpose(upper, (3, 2, 0, 1, 4)).reshape(2, freq_local, receivers, receivers)
    mirror = jnp.swapaxes(upper, 2, 3)
    mirror = jnp.stack([mirror[0], -mirror[1]])
    row_tile = lax.broadcasted_iota(jnp.int32, (tiles, 1, tiles, 1), 0)
    col_tile = lax.broadcasted_iota(jnp.int32, (tiles, 1, tiles, 1), 2)
    direct = (col_tile - row_tile) % tiles <= tiles // 2
    shape6 = (2, freq_local, tiles, tile, tiles, tile)
    whole = jnp.where(direct, upper.reshape(shape6), mirror.reshape(shape6))
    return whole.reshape(upper.shape)


def per_device(downgoing, upgoing, source_order):
    shot_count = lax.axis_size("shot")
    core_count = lax.axis_size("sub")
    core_index = lax.axis_index("sub")
    receivers = downgoing.shape[3]
    freq_local = downgoing.shape[1]
    sources = source_order.shape[0]
    groups = shot_count * core_count
    source_local = sources // groups
    rows_each = receivers // groups
    tiles = 8 if groups % 8 == 0 else groups
    tile = receivers // tiles
    span = (tiles // 2 + 1) * tile

    right = stacked_right(downgoing)

    left = stacked_rows(downgoing).reshape(freq_local, 2, shot_count, core_count, rows_each, -1)
    left = lax.dynamic_slice_in_dim(left, core_index, 1, 3)[:, :, :, 0]
    gram_rows = jnp.einsum("qpkit,qto->kiqpo", left, right, preferred_element_type=jnp.float32)
    gram_part = strip_partials(gram_rows, shot_count, core_count, core_index, rows_each, tile, span)
    gram_strip = lax.psum_scatter(gram_part, "shot", scatter_dimension=0, tiled=True)

    corr_all = jnp.einsum(
        "qtpu,qto->uqpo", stacked_left(upgoing), right, preferred_element_type=jnp.float32
    )
    order_table = source_order.reshape(shot_count, core_count, source_local)
    own_order = lax.dynamic_slice_in_dim(order_table, core_index, 1, 1).reshape(-1)
    corr_part = jnp.take(corr_all, own_order, axis=0).astype(jnp.bfloat16)

    gram_strip, corr_part, power_trace = lax.optimization_barrier((gram_strip, corr_part, downgoing))

    shot_index = lax.axis_index("shot")
    corr_blocks = corr_part.reshape(shot_count, source_local, *corr_part.shape[1:])
    corr = lax.dynamic_index_in_dim(corr_blocks, shot_index, 0, keepdims=False).astype(jnp.float32)
    for shift in range(1, shot_count):
        outgoing = lax.dynamic_index_in_dim(corr_blocks, (shot_index + shift) % shot_count, 0, keepdims=False)
        pairs = [(k, (k + shift) % shot_count) for k in range(shot_count)]
        corr = corr + lax.ppermute(outgoing, "shot", perm=pairs).astype(jnp.float32)

    across = lax.all_gather(gram_strip, "shot", axis=0, tiled=True)
    across = across.reshape(shot_count, rows_each, freq_local, 2, span)
    local_power = jnp.sum(jnp.square(power_trace.astype(jnp.float32)), axis=(0, 2, 3))
    power = lax.psum(local_power, "shot") / receivers
    across, power = lax.optimization_barrier((across, power))
    power_wide = power[None, :, None, None]

    if core_count == 2:
        other = lax.ppermute(across, "sub", perm=[(0, 1), (1, 0)])
        first = jnp.where(core_index == 0, across, other)
        second = jnp.where(core_index == 0, other, across)
        strips = jnp.stack([first, second], axis=1)
    else:
        strips = lax.all_gather(across, "sub", axis=1, tiled=False)
    strips = strips.reshape(receivers, freq_local, 2, span)
    whole = rebuild_gram(strips, tiles, tile)

    target = jnp.transpose(corr, (2, 1, 0, 3)) / power_wide

    scaled = (whole.astype(jnp.float32) / power_wide).astype(jnp.bfloat16)
    solution = jnp.zeros((2, freq_local, source_local, receivers), jnp.float32)
    return sweep_whole(scaled, solution, target)


def solution(mesh):
    return jax.shard_map(
        per_device,
        mesh=mesh,
        in_specs=(
            P(None, "freq", ("grp", "shot"), None),
            P(None, "freq", ("grp", "shot"), None),
            P("grp"),
        ),
        out_specs=P(None, "freq", ("grp", "shot", "sub"), None),
        check_vma=False,
    )
```

```python
import jax
import jax.numpy as jnp
from jax import lax
from jax.sharding import PartitionSpec as P

SWEEPS = 6


relaxation = 0.125
damping = 1.0


def stacked_rows(factor):
    real_left = jnp.concatenate([factor[0], factor[1]], axis=1)
    imag_left = jnp.concatenate([factor[1], -factor[0]], axis=1)
    return jnp.swapaxes(jnp.stack([real_left, imag_left], axis=1), 2, 3)


def stacked_left(factor):
    real_left = jnp.concatenate([factor[0], factor[1]], axis=1)
    imag_left = jnp.concatenate([factor[1], -factor[0]], axis=1)
    return jnp.stack([real_left, imag_left], axis=2)


def stacked_right(trace):
    return jnp.concatenate([trace[0], trace[1]], axis=1)


def sweep_whole(wide, solution, target):
    receivers = target.shape[-1]
    sources = target.shape[2]
    for sweep in range(SWEEPS):
        narrow = solution.astype(jnp.bfloat16)
        stacked = jnp.concatenate([narrow[0], narrow[1]], axis=1)
        products = jnp.einsum("qjc,qcr->qjr", stacked, wide, preferred_element_type=jnp.float32)
        real_real = products[:, :sources, :receivers]
        real_imag = products[:, :sources, receivers:]
        imag_real = products[:, sources:, :receivers]
        imag_imag = products[:, sources:, receivers:]
        image = jnp.stack([real_real - imag_imag, real_imag + imag_real])
        solution = solution + relaxation * (target - image - damping * solution)
    return solution


def strip_partials(rows, shot_count, core_count, core_index, rows_each, tile, span):
    rows = rows.astype(jnp.bfloat16)
    doubled = jnp.concatenate([rows, rows], axis=-1)
    windows = []
    for k in range(shot_count):
        start = ((k * core_count + core_index) * rows_each // tile) * tile
        windows.append(lax.dynamic_slice_in_dim(doubled[k], start, span, axis=-1))
    return jnp.stack(windows).reshape(shot_count * rows_each, *rows.shape[2:4], span)


def rebuild_gram(strips, tiles, tile):
    freq_local = strips.shape[1]
    receivers = tiles * tile
    span = strips.shape[-1]
    padded = jnp.pad(strips, [(0, 0)] * 3 + [(0, receivers - span)])
    padded = padded.reshape(tiles, tile, freq_local, 2, receivers)
    upper = jnp.stack([jnp.roll(padded[a], a * tile, axis=-1) for a in range(tiles)])
    upper = jnp.transpose(upper, (2, 0, 1, 3, 4)).reshape(freq_local, receivers, 2, receivers)
    mirror = jnp.transpose(upper, (0, 3, 2, 1))
    mirror = jnp.stack([mirror[:, :, 0], -mirror[:, :, 1]], axis=2)
    row_tile = lax.broadcasted_iota(jnp.int32, (tiles, 1, 1, tiles, 1), 0)
    col_tile = lax.broadcasted_iota(jnp.int32, (tiles, 1, 1, tiles, 1), 3)
    direct = (col_tile - row_tile) % tiles <= tiles // 2
    shape6 = (freq_local, tiles, tile, 2, tiles, tile)
    whole = jnp.where(direct, upper.reshape(shape6), mirror.reshape(shape6))
    return whole.reshape(upper.shape)


def per_device(downgoing, upgoing, source_order):
    shot_count = lax.axis_size("shot")
    core_count = lax.axis_size("sub")
    core_index = lax.axis_index("sub")
    receivers = downgoing.shape[3]
    freq_local = downgoing.shape[1]
    sources = source_order.shape[0]
    groups = shot_count * core_count
    source_local = sources // groups
    rows_each = receivers // groups
    tiles = 8 if groups % 8 == 0 else groups
    tile = receivers // tiles
    span = (tiles // 2 + 1) * tile

    right = stacked_right(downgoing)

    left = stacked_rows(downgoing).reshape(freq_local, 2, shot_count, core_count, rows_each, -1)
    left = lax.dynamic_slice_in_dim(left, core_index, 1, 3)[:, :, :, 0]
    gram_rows = jnp.einsum("qpkit,qto->kiqpo", left, right, preferred_element_type=jnp.float32)
    gram_part = strip_partials(gram_rows, shot_count, core_count, core_index, rows_each, tile, span)
    gram_strip = lax.psum_scatter(gram_part, "shot", scatter_dimension=0, tiled=True)

    corr_all = jnp.einsum(
        "qtpu,qto->uqpo", stacked_left(upgoing), right, preferred_element_type=jnp.float32
    )
    order_table = source_order.reshape(shot_count, core_count, source_local)
    own_order = lax.dynamic_slice_in_dim(order_table, core_index, 1, 1).reshape(-1)
    corr_part = jnp.take(corr_all, own_order, axis=0).astype(jnp.bfloat16)

    gram_strip, corr_part, power_trace = lax.optimization_barrier((gram_strip, corr_part, downgoing))

    shot_index = lax.axis_index("shot")
    corr_blocks = corr_part.reshape(shot_count, source_local, *corr_part.shape[1:])
    corr = lax.dynamic_index_in_dim(corr_blocks, shot_index, 0, keepdims=False).astype(jnp.float32)
    for shift in range(1, shot_count):
        outgoing = lax.dynamic_index_in_dim(corr_blocks, (shot_index + shift) % shot_count, 0, keepdims=False)
        pairs = [(k, (k + shift) % shot_count) for k in range(shot_count)]
        corr = corr + lax.ppermute(outgoing, "shot", perm=pairs).astype(jnp.float32)

    across = lax.all_gather(gram_strip, "shot", axis=0, tiled=True)
    across = across.reshape(shot_count, rows_each, freq_local, 2, span)
    local_power = jnp.sum(jnp.square(power_trace.astype(jnp.float32)), axis=(0, 2, 3))
    power = lax.psum(local_power, "shot") / receivers
    across, power = lax.optimization_barrier((across, power))
    power_wide = power[None, :, None, None]

    if core_count == 2:
        other = lax.ppermute(across, "sub", perm=[(0, 1), (1, 0)])
        first = jnp.where(core_index == 0, across, other)
        second = jnp.where(core_index == 0, other, across)
        strips = jnp.stack([first, second], axis=1)
    else:
        strips = lax.all_gather(across, "sub", axis=1, tiled=False)
    strips = strips.reshape(receivers, freq_local, 2, span)
    whole = rebuild_gram(strips, tiles, tile)

    target = jnp.transpose(corr, (2, 1, 0, 3)) / power_wide

    scaled = (whole.astype(jnp.float32) / power[:, None, None, None]).astype(jnp.bfloat16)
    scaled = scaled.reshape(freq_local, receivers, 2 * receivers)
    solution = jnp.zeros((2, freq_local, source_local, receivers), jnp.float32)
    return sweep_whole(scaled, solution, target)


def solution(mesh):
    return jax.shard_map(
        per_device,
        mesh=mesh,
        in_specs=(
            P(None, "freq", ("grp", "shot"), None),
            P(None, "freq", ("grp", "shot"), None),
            P("grp"),
        ),
        out_specs=P(None, "freq", ("grp", "shot", "sub"), None),
        check_vma=False,
    )
```

```python
import jax
import jax.numpy as jnp
from jax import lax
from jax.sharding import PartitionSpec as P

SWEEPS = 6


relaxation = 0.125
damping = 1.0


def stacked_rows(factor):
    real_left = jnp.concatenate([factor[0], factor[1]], axis=1)
    imag_left = jnp.concatenate([factor[1], -factor[0]], axis=1)
    return jnp.swapaxes(jnp.stack([real_left, imag_left], axis=1), 2, 3)


def stacked_left(factor):
    real_left = jnp.concatenate([factor[0], factor[1]], axis=1)
    imag_left = jnp.concatenate([factor[1], -factor[0]], axis=1)
    return jnp.stack([real_left, imag_left], axis=2)


def stacked_right(trace):
    return jnp.concatenate([trace[0], trace[1]], axis=1)


def sweep_whole(scaled, solution, target):
    receivers = target.shape[-1]
    sources = target.shape[2]
    wide = jnp.concatenate([scaled[0], scaled[1]], axis=-1)
    for sweep in range(SWEEPS):
        narrow = solution.astype(jnp.bfloat16)
        stacked = jnp.concatenate([narrow[0], narrow[1]], axis=1)
        products = jnp.einsum("qjc,qcr->qjr", stacked, wide, preferred_element_type=jnp.float32)
        real_real = products[:, :sources, :receivers]
        real_imag = products[:, :sources, receivers:]
        imag_real = products[:, sources:, :receivers]
        imag_imag = products[:, sources:, receivers:]
        image = jnp.stack([real_real - imag_imag, real_imag + imag_real])
        solution = solution + relaxation * (target - image - damping * solution)
    return solution


def strip_partials(rows, shot_count, core_count, core_index, rows_each, tile, span):
    rows = rows.astype(jnp.bfloat16)
    doubled = jnp.concatenate([rows, rows], axis=-1)
    windows = []
    for k in range(shot_count):
        start = ((k * core_count + core_index) * rows_each // tile) * tile
        windows.append(lax.dynamic_slice_in_dim(doubled[k], start, span, axis=-1))
    return jnp.stack(windows).reshape(shot_count * rows_each, *rows.shape[2:4], span)


def rebuild_gram(strips, tiles, tile):
    freq_local = strips.shape[1]
    receivers = tiles * tile
    span = strips.shape[-1]
    padded = jnp.pad(strips, [(0, 0)] * 3 + [(0, receivers - span)])
    padded = padded.reshape(tiles, tile, freq_local, 2, receivers)
    upper = jnp.stack([jnp.roll(padded[a], a * tile, axis=-1) for a in range(tiles)])
    upper = jnp.transpose(upper, (3, 2, 0, 1, 4)).reshape(2, freq_local, receivers, receivers)
    mirror = jnp.swapaxes(upper, 2, 3)
    mirror = jnp.stack([mirror[0], -mirror[1]])
    row_tile = lax.broadcasted_iota(jnp.int32, (tiles, 1, tiles, 1), 0)
    col_tile = lax.broadcasted_iota(jnp.int32, (tiles, 1, tiles, 1), 2)
    direct = (col_tile - row_tile) % tiles <= tiles // 2
    shape6 = (2, freq_local, tiles, tile, tiles, tile)
    whole = jnp.where(direct, upper.reshape(shape6), mirror.reshape(shape6))
    return whole.reshape(upper.shape)


def per_device(downgoing, upgoing, source_order):
    shot_count = lax.axis_size("shot")
    core_count = lax.axis_size("sub")
    core_index = lax.axis_index("sub")
    receivers = downgoing.shape[3]
    freq_local = downgoing.shape[1]
    sources = source_order.shape[0]
    groups = shot_count * core_count
    source_local = sources // groups
    rows_each = receivers // groups
    tiles = 8 if groups % 8 == 0 else groups
    tile = receivers // tiles
    span = (tiles // 2 + 1) * tile

    right = stacked_right(downgoing)

    left = stacked_rows(downgoing).reshape(freq_local, 2, shot_count, core_count, rows_each, -1)
    left = lax.dynamic_slice_in_dim(left, core_index, 1, 3)[:, :, :, 0]
    gram_rows = jnp.einsum("qpkit,qto->kiqpo", left, right, preferred_element_type=jnp.float32)
    gram_part = strip_partials(gram_rows, shot_count, core_count, core_index, rows_each, tile, span)
    gram_strip = lax.psum_scatter(gram_part, "shot", scatter_dimension=0, tiled=True)

    corr_all = jnp.einsum(
        "qtpu,qto->uqpo", stacked_left(upgoing), right, preferred_element_type=jnp.float32
    )
    order_table = source_order.reshape(shot_count, core_count, source_local)
    own_order = lax.dynamic_slice_in_dim(order_table, core_index, 1, 1).reshape(-1)
    corr_part = jnp.take(corr_all, own_order, axis=0).astype(jnp.bfloat16)

    gram_strip, corr_part, power_trace = lax.optimization_barrier((gram_strip, corr_part, downgoing))

    shot_index = lax.axis_index("shot")
    corr_blocks = corr_part.reshape(shot_count, source_local, *corr_part.shape[1:])
    corr = lax.dynamic_index_in_dim(corr_blocks, shot_index, 0, keepdims=False).astype(jnp.float32)
    for shift in range(1, shot_count):
        outgoing = lax.dynamic_index_in_dim(corr_blocks, (shot_index + shift) % shot_count, 0, keepdims=False)
        pairs = [(k, (k + shift) % shot_count) for k in range(shot_count)]
        corr = corr + lax.ppermute(outgoing, "shot", perm=pairs).astype(jnp.float32)

    across = lax.all_gather(gram_strip, "shot", axis=0, tiled=True)
    across = across.reshape(shot_count, rows_each, freq_local, 2, span)
    local_power = jnp.sum(jnp.square(power_trace.astype(jnp.float32)), axis=(0, 2, 3))
    power = lax.psum(local_power, "shot") / receivers
    across, power = lax.optimization_barrier((across, power))
    power_wide = power[None, :, None, None]

    if core_count == 2:
        other = lax.ppermute(across, "sub", perm=[(0, 1), (1, 0)])
        first = jnp.where(core_index == 0, across, other)
        second = jnp.where(core_index == 0, other, across)
        strips = jnp.stack([first, second], axis=1)
    else:
        strips = lax.all_gather(across, "sub", axis=1, tiled=False)
    strips = strips.reshape(receivers, freq_local, 2, span)
    whole = rebuild_gram(strips, tiles, tile)

    target = jnp.transpose(corr, (2, 1, 0, 3)) / power_wide

    scaled = (whole.astype(jnp.float32) / power_wide).astype(jnp.bfloat16)
    solution = jnp.zeros((2, freq_local, source_local, receivers), jnp.float32)
    return sweep_whole(scaled, solution, target)


def solution(mesh):
    return jax.shard_map(
        per_device,
        mesh=mesh,
        in_specs=(
            P(None, "freq", ("grp", "shot"), None),
            P(None, "freq", ("grp", "shot"), None),
            P("grp"),
        ),
        out_specs=P(None, "freq", ("grp", "shot", "sub"), None),
        check_vma=False,
    )
```

```python
import jax
import jax.numpy as jnp
from jax import lax
from jax.sharding import PartitionSpec as P

SWEEPS = 6


relaxation = 0.125
damping = 1.0


def stacked_rows(factor):
    real_left = jnp.concatenate([factor[0], factor[1]], axis=1)
    imag_left = jnp.concatenate([factor[1], -factor[0]], axis=1)
    return jnp.swapaxes(jnp.stack([real_left, imag_left], axis=1), 2, 3)


def stacked_left(factor):
    real_left = jnp.concatenate([factor[0], factor[1]], axis=1)
    imag_left = jnp.concatenate([factor[1], -factor[0]], axis=1)
    return jnp.stack([real_left, imag_left], axis=2)


def stacked_right(trace):
    return jnp.concatenate([trace[0], trace[1]], axis=1)


def sweep_whole(scaled, solution, target):
    receivers = target.shape[-1]
    sources = target.shape[2]
    wide = jnp.concatenate([scaled[0], scaled[1]], axis=-1)
    for sweep in range(SWEEPS):
        narrow = solution.astype(jnp.bfloat16)
        stacked = jnp.concatenate([narrow[0], narrow[1]], axis=1)
        products = jnp.einsum("qjc,qcr->qjr", stacked, wide, preferred_element_type=jnp.float32)
        real_real = products[:, :sources, :receivers]
        real_imag = products[:, :sources, receivers:]
        imag_real = products[:, sources:, :receivers]
        imag_imag = products[:, sources:, receivers:]
        image = jnp.stack([real_real - imag_imag, real_imag + imag_real])
        solution = solution + relaxation * (target - image - damping * solution)
    return solution


def strip_partials(rows, shot_count, core_count, core_index, rows_each, tile, span):
    rows = rows.astype(jnp.bfloat16)
    doubled = jnp.concatenate([rows, rows], axis=-1)
    windows = []
    for k in range(shot_count):
        start = ((k * core_count + core_index) * rows_each // tile) * tile
        windows.append(lax.dynamic_slice_in_dim(doubled[k], start, span, axis=-1))
    return jnp.stack(windows).reshape(shot_count * rows_each, *rows.shape[2:4], span)


def rebuild_gram(strips, tiles, tile):
    freq_local = strips.shape[1]
    receivers = tiles * tile
    span = strips.shape[-1]
    padded = jnp.pad(strips, [(0, 0)] * 3 + [(0, receivers - span)])
    padded = padded.reshape(tiles, tile, freq_local, 2, receivers)
    upper = jnp.stack([jnp.roll(padded[a], a * tile, axis=-1) for a in range(tiles)])
    upper = jnp.transpose(upper, (3, 2, 0, 1, 4)).reshape(2, freq_local, receivers, receivers)
    mirror = jnp.swapaxes(upper, 2, 3)
    mirror = jnp.stack([mirror[0], -mirror[1]])
    row_tile = lax.broadcasted_iota(jnp.int32, (tiles, 1, tiles, 1), 0)
    col_tile = lax.broadcasted_iota(jnp.int32, (tiles, 1, tiles, 1), 2)
    direct = (col_tile - row_tile) % tiles <= tiles // 2
    shape6 = (2, freq_local, tiles, tile, tiles, tile)
    whole = jnp.where(direct, upper.reshape(shape6), mirror.reshape(shape6))
    return whole.reshape(upper.shape)


def per_device(downgoing, upgoing, source_order):
    shot_count = lax.axis_size("shot")
    core_count = lax.axis_size("sub")
    core_index = lax.axis_index("sub")
    receivers = downgoing.shape[3]
    freq_local = downgoing.shape[1]
    sources = source_order.shape[0]
    groups = shot_count * core_count
    source_local = sources // groups
    rows_each = receivers // groups
    tiles = 8 if groups % 8 == 0 else groups
    tile = receivers // tiles
    span = (tiles // 2 + 1) * tile

    right = stacked_right(downgoing)

    left = stacked_rows(downgoing).reshape(freq_local, 2, shot_count, core_count, rows_each, -1)
    left = lax.dynamic_slice_in_dim(left, core_index, 1, 3)[:, :, :, 0]
    gram_rows = jnp.einsum("qpkit,qto->kiqpo", left, right, preferred_element_type=jnp.float32)
    gram_part = strip_partials(gram_rows, shot_count, core_count, core_index, rows_each, tile, span)
    gram_strip = lax.psum_scatter(gram_part, "shot", scatter_dimension=0, tiled=True)

    corr_all = jnp.einsum(
        "qtpu,qto->uqpo", stacked_left(upgoing), right, preferred_element_type=jnp.float32
    )
    order_table = source_order.reshape(shot_count, core_count, source_local)
    own_order = lax.dynamic_slice_in_dim(order_table, core_index, 1, 1).reshape(-1)
    corr_part = jnp.take(corr_all, own_order, axis=0).astype(jnp.bfloat16)

    gram_strip, corr_part, power_trace = lax.optimization_barrier((gram_strip, corr_part, downgoing))

    shot_index = lax.axis_index("shot")
    corr_blocks = corr_part.reshape(shot_count, source_local, *corr_part.shape[1:])
    corr = lax.dynamic_index_in_dim(corr_blocks, shot_index, 0, keepdims=False).astype(jnp.float32)
    for shift in range(1, shot_count):
        outgoing = lax.dynamic_index_in_dim(corr_blocks, (shot_index + shift) % shot_count, 0, keepdims=False)
        pairs = [(k, (k + shift) % shot_count) for k in range(shot_count)]
        corr = corr + lax.ppermute(outgoing, "shot", perm=pairs).astype(jnp.float32)

    strips = lax.all_gather(gram_strip, ("shot", "sub"), axis=0, tiled=True)
    local_power = jnp.sum(jnp.square(power_trace.astype(jnp.float32)), axis=(0, 2, 3))
    power = lax.psum(local_power, "shot") / receivers
    strips, power = lax.optimization_barrier((strips, power))
    power_wide = power[None, :, None, None]
    strips = strips.reshape(receivers, freq_local, 2, span)
    whole = rebuild_gram(strips, tiles, tile)

    target = jnp.transpose(corr, (2, 1, 0, 3)) / power_wide

    scaled = (whole.astype(jnp.float32) / power_wide).astype(jnp.bfloat16)
    solution = jnp.zeros((2, freq_local, source_local, receivers), jnp.float32)
    return sweep_whole(scaled, solution, target)


def solution(mesh):
    return jax.shard_map(
        per_device,
        mesh=mesh,
        in_specs=(
            P(None, "freq", ("grp", "shot"), None),
            P(None, "freq", ("grp", "shot"), None),
            P("grp"),
        ),
        out_specs=P(None, "freq", ("grp", "shot", "sub"), None),
        check_vma=False,
    )
```

```python
import jax
import jax.numpy as jnp
from jax import lax
from jax.sharding import PartitionSpec as P

SWEEPS = 6


relaxation = 0.125
damping = 1.0


def stacked_rows(factor):
    real_left = jnp.concatenate([factor[0], factor[1]], axis=1)
    imag_left = jnp.concatenate([factor[1], -factor[0]], axis=1)
    return jnp.swapaxes(jnp.stack([real_left, imag_left], axis=1), 2, 3)


def stacked_left(factor):
    real_left = jnp.concatenate([factor[0], factor[1]], axis=1)
    imag_left = jnp.concatenate([factor[1], -factor[0]], axis=1)
    return jnp.stack([real_left, imag_left], axis=2)


def stacked_right(trace):
    return jnp.concatenate([trace[0], trace[1]], axis=1)


def sweep_whole(scaled, solution, target):
    receivers = target.shape[-1]
    sources = target.shape[2]
    wide = jnp.concatenate([scaled[0], scaled[1]], axis=-1)
    for sweep in range(SWEEPS):
        narrow = solution.astype(jnp.bfloat16)
        stacked = jnp.concatenate([narrow[0], narrow[1]], axis=1)
        products = jnp.einsum("qjc,qcr->qjr", stacked, wide, preferred_element_type=jnp.float32)
        real_real = products[:, :sources, :receivers]
        real_imag = products[:, :sources, receivers:]
        imag_real = products[:, sources:, :receivers]
        imag_imag = products[:, sources:, receivers:]
        image = jnp.stack([real_real - imag_imag, real_imag + imag_real])
        solution = solution + relaxation * (target - image - damping * solution)
    return solution


def strip_partials(rows, shot_count, core_count, core_index, rows_each, tile, span):
    receivers = rows.shape[-1]
    rows = rows.astype(jnp.bfloat16)

    def window(k, start):
        if start + span <= receivers:
            return rows[k, ..., start : start + span]
        return jnp.concatenate([rows[k, ..., start:], rows[k, ..., : start + span - receivers]], axis=-1)

    windows = []
    for k in range(shot_count):
        chosen = window(k, (k * core_count * rows_each // tile) * tile)
        for position in range(1, core_count):
            start = ((k * core_count + position) * rows_each // tile) * tile
            chosen = jnp.where(core_index == position, window(k, start), chosen)
        windows.append(chosen)
    return jnp.stack(windows).reshape(shot_count * rows_each, *rows.shape[2:4], span)


def rebuild_gram(strips, tiles, tile):
    freq_local = strips.shape[1]
    receivers = tiles * tile
    span = strips.shape[-1]
    padded = jnp.pad(strips, [(0, 0)] * 3 + [(0, receivers - span)])
    padded = padded.reshape(tiles, tile, freq_local, 2, receivers)
    upper = jnp.stack([jnp.roll(padded[a], a * tile, axis=-1) for a in range(tiles)])
    upper = jnp.transpose(upper, (3, 2, 0, 1, 4)).reshape(2, freq_local, receivers, receivers)
    mirror = jnp.swapaxes(upper, 2, 3)
    mirror = jnp.stack([mirror[0], -mirror[1]])
    row_tile = lax.broadcasted_iota(jnp.int32, (tiles, 1, tiles, 1), 0)
    col_tile = lax.broadcasted_iota(jnp.int32, (tiles, 1, tiles, 1), 2)
    direct = (col_tile - row_tile) % tiles <= tiles // 2
    shape6 = (2, freq_local, tiles, tile, tiles, tile)
    whole = jnp.where(direct, upper.reshape(shape6), mirror.reshape(shape6))
    return whole.reshape(upper.shape)


def per_device(downgoing, upgoing, source_order):
    shot_count = lax.axis_size("shot")
    core_count = lax.axis_size("sub")
    core_index = lax.axis_index("sub")
    receivers = downgoing.shape[3]
    freq_local = downgoing.shape[1]
    sources = source_order.shape[0]
    groups = shot_count * core_count
    source_local = sources // groups
    rows_each = receivers // groups
    tiles = 8 if groups % 8 == 0 else groups
    tile = receivers // tiles
    span = (tiles // 2 + 1) * tile

    right = stacked_right(downgoing)

    left = stacked_rows(downgoing).reshape(freq_local, 2, shot_count, core_count, rows_each, -1)
    left = lax.dynamic_slice_in_dim(left, core_index, 1, 3)[:, :, :, 0]
    gram_rows = jnp.einsum("qpkit,qto->kiqpo", left, right, preferred_element_type=jnp.float32)
    gram_part = strip_partials(gram_rows, shot_count, core_count, core_index, rows_each, tile, span)
    gram_strip = lax.psum_scatter(gram_part, "shot", scatter_dimension=0, tiled=True)

    corr_all = jnp.einsum(
        "qtpu,qto->uqpo", stacked_left(upgoing), right, preferred_element_type=jnp.float32
    )
    order_table = source_order.reshape(shot_count, core_count, source_local)
    own_order = lax.dynamic_slice_in_dim(order_table, core_index, 1, 1).reshape(-1)
    corr_part = jnp.take(corr_all, own_order, axis=0).astype(jnp.bfloat16)

    gram_strip, corr_part, power_trace = lax.optimization_barrier((gram_strip, corr_part, downgoing))

    shot_index = lax.axis_index("shot")
    corr_blocks = corr_part.reshape(shot_count, source_local, *corr_part.shape[1:])
    corr = lax.dynamic_index_in_dim(corr_blocks, shot_index, 0, keepdims=False).astype(jnp.float32)
    for shift in range(1, shot_count):
        outgoing = lax.dynamic_index_in_dim(corr_blocks, (shot_index + shift) % shot_count, 0, keepdims=False)
        pairs = [(k, (k + shift) % shot_count) for k in range(shot_count)]
        corr = corr + lax.ppermute(outgoing, "shot", perm=pairs).astype(jnp.float32)

    across = lax.all_gather(gram_strip, "shot", axis=0, tiled=True)
    across = across.reshape(shot_count, rows_each, freq_local, 2, span)
    local_power = jnp.sum(jnp.square(power_trace.astype(jnp.float32)), axis=(0, 2, 3))
    power = lax.psum(local_power, "shot") / receivers
    across, power = lax.optimization_barrier((across, power))
    power_wide = power[None, :, None, None]

    if core_count == 2:
        other = lax.ppermute(across, "sub", perm=[(0, 1), (1, 0)])
        first = jnp.where(core_index == 0, across, other)
        second = jnp.where(core_index == 0, other, across)
        strips = jnp.stack([first, second], axis=1)
    else:
        strips = lax.all_gather(across, "sub", axis=1, tiled=False)
    strips = strips.reshape(receivers, freq_local, 2, span)
    whole = rebuild_gram(strips, tiles, tile)

    target = jnp.transpose(corr, (2, 1, 0, 3)) / power_wide

    scaled = (whole.astype(jnp.float32) / power_wide).astype(jnp.bfloat16)
    solution = jnp.zeros((2, freq_local, source_local, receivers), jnp.float32)
    return sweep_whole(scaled, solution, target)


def solution(mesh):
    return jax.shard_map(
        per_device,
        mesh=mesh,
        in_specs=(
            P(None, "freq", ("grp", "shot"), None),
            P(None, "freq", ("grp", "shot"), None),
            P("grp"),
        ),
        out_specs=P(None, "freq", ("grp", "shot", "sub"), None),
        check_vma=False,
    )
```

```python
import jax
import jax.numpy as jnp
from jax import lax
from jax.sharding import PartitionSpec as P

SWEEPS = 6


relaxation = 0.125
damping = 1.0


def stacked_rows(factor):
    real_left = jnp.concatenate([factor[0], factor[1]], axis=1)
    imag_left = jnp.concatenate([factor[1], -factor[0]], axis=1)
    return jnp.swapaxes(jnp.stack([real_left, imag_left], axis=1), 2, 3)


def stacked_left(factor):
    real_left = jnp.concatenate([factor[0], factor[1]], axis=1)
    imag_left = jnp.concatenate([factor[1], -factor[0]], axis=1)
    return jnp.stack([real_left, imag_left], axis=2)


def stacked_right(trace):
    return jnp.concatenate([trace[0], trace[1]], axis=1)


def sweep_whole(scaled, solution, target):
    receivers = target.shape[-1]
    sources = target.shape[2]
    wide = jnp.concatenate([scaled[0], scaled[1]], axis=-1)
    for sweep in range(SWEEPS):
        narrow = solution.astype(jnp.bfloat16)
        stacked = jnp.concatenate([narrow[0], narrow[1]], axis=1)
        products = jnp.einsum("qjc,qcr->qjr", stacked, wide, preferred_element_type=jnp.float32)
        real_real = products[:, :sources, :receivers]
        real_imag = products[:, :sources, receivers:]
        imag_real = products[:, sources:, :receivers]
        imag_imag = products[:, sources:, receivers:]
        image = jnp.stack([real_real - imag_imag, real_imag + imag_real])
        solution = solution + relaxation * (target - image - damping * solution)
    return solution


def strip_partials(rows, shot_count, core_count, core_index, rows_each, tile, span):
    rows = rows.astype(jnp.bfloat16)
    doubled = jnp.concatenate([rows, rows], axis=-1)
    windows = []
    for k in range(shot_count):
        start = ((k * core_count + core_index) * rows_each // tile) * tile
        windows.append(lax.dynamic_slice_in_dim(doubled[k], start, span, axis=-1))
    return jnp.stack(windows).reshape(shot_count * rows.shape[1], *rows.shape[2:4], span)


def rebuild_gram(strips, tiles, tile):
    freq_local = strips.shape[1]
    receivers = tiles * tile
    span = strips.shape[-1]
    padded = jnp.pad(strips, [(0, 0)] * 3 + [(0, receivers - span)])
    padded = padded.reshape(tiles, tile, freq_local, 2, receivers)
    upper = jnp.stack([jnp.roll(padded[a], a * tile, axis=-1) for a in range(tiles)])
    upper = jnp.transpose(upper, (3, 2, 0, 1, 4)).reshape(2, freq_local, receivers, receivers)
    mirror = jnp.swapaxes(upper, 2, 3)
    mirror = jnp.stack([mirror[0], -mirror[1]])
    row_tile = lax.broadcasted_iota(jnp.int32, (tiles, 1, tiles, 1), 0)
    col_tile = lax.broadcasted_iota(jnp.int32, (tiles, 1, tiles, 1), 2)
    direct = (col_tile - row_tile) % tiles <= tiles // 2
    shape6 = (2, freq_local, tiles, tile, tiles, tile)
    whole = jnp.where(direct, upper.reshape(shape6), mirror.reshape(shape6))
    return whole.reshape(upper.shape)


def per_device(downgoing, upgoing, source_order):
    shot_count = lax.axis_size("shot")
    core_count = lax.axis_size("sub")
    core_index = lax.axis_index("sub")
    receivers = downgoing.shape[3]
    freq_local = downgoing.shape[1]
    sources = source_order.shape[0]
    groups = shot_count * core_count
    source_local = sources // groups
    rows_each = receivers // groups
    tiles = 8 if groups % 8 == 0 else groups
    tile = receivers // tiles
    span = (tiles // 2 + 1) * tile

    right = stacked_right(downgoing)

    left = stacked_rows(downgoing).reshape(freq_local, 2, shot_count, core_count, rows_each, -1)
    left = lax.dynamic_slice_in_dim(left, core_index, 1, 3)[:, :, :, 0]
    half = rows_each // 2 if rows_each % 16 == 0 else rows_each
    chunks = []
    for low in range(0, rows_each, half):
        chunk_rows = jnp.einsum(
            "qpkit,qto->kiqpo", left[:, :, :, low : low + half], right, preferred_element_type=jnp.float32
        )
        chunk_part = strip_partials(chunk_rows, shot_count, core_count, core_index, rows_each, tile, span)
        chunks.append(lax.psum_scatter(chunk_part, "shot", scatter_dimension=0, tiled=True))
    gram_strip = jnp.concatenate(chunks, axis=0)

    corr_all = jnp.einsum(
        "qtpu,qto->uqpo", stacked_left(upgoing), right, preferred_element_type=jnp.float32
    )
    order_table = source_order.reshape(shot_count, core_count, source_local)
    own_order = lax.dynamic_slice_in_dim(order_table, core_index, 1, 1).reshape(-1)
    corr_part = jnp.take(corr_all, own_order, axis=0).astype(jnp.bfloat16)

    gram_strip, corr_part, power_trace = lax.optimization_barrier((gram_strip, corr_part, downgoing))

    shot_index = lax.axis_index("shot")
    corr_blocks = corr_part.reshape(shot_count, source_local, *corr_part.shape[1:])
    corr = lax.dynamic_index_in_dim(corr_blocks, shot_index, 0, keepdims=False).astype(jnp.float32)
    for shift in range(1, shot_count):
        outgoing = lax.dynamic_index_in_dim(corr_blocks, (shot_index + shift) % shot_count, 0, keepdims=False)
        pairs = [(k, (k + shift) % shot_count) for k in range(shot_count)]
        corr = corr + lax.ppermute(outgoing, "shot", perm=pairs).astype(jnp.float32)

    across = lax.all_gather(gram_strip, "shot", axis=0, tiled=True)
    across = across.reshape(shot_count, rows_each, freq_local, 2, span)
    local_power = jnp.sum(jnp.square(power_trace.astype(jnp.float32)), axis=(0, 2, 3))
    power = lax.psum(local_power, "shot") / receivers
    across, power = lax.optimization_barrier((across, power))
    power_wide = power[None, :, None, None]

    if core_count == 2:
        other = lax.ppermute(across, "sub", perm=[(0, 1), (1, 0)])
        first = jnp.where(core_index == 0, across, other)
        second = jnp.where(core_index == 0, other, across)
        strips = jnp.stack([first, second], axis=1)
    else:
        strips = lax.all_gather(across, "sub", axis=1, tiled=False)
    strips = strips.reshape(receivers, freq_local, 2, span)
    whole = rebuild_gram(strips, tiles, tile)

    target = jnp.transpose(corr, (2, 1, 0, 3)) / power_wide

    scaled = (whole.astype(jnp.float32) / power_wide).astype(jnp.bfloat16)
    solution = jnp.zeros((2, freq_local, source_local, receivers), jnp.float32)
    return sweep_whole(scaled, solution, target)


def solution(mesh):
    return jax.shard_map(
        per_device,
        mesh=mesh,
        in_specs=(
            P(None, "freq", ("grp", "shot"), None),
            P(None, "freq", ("grp", "shot"), None),
            P("grp"),
        ),
        out_specs=P(None, "freq", ("grp", "shot", "sub"), None),
        check_vma=False,
    )
```

```python
import jax
import jax.numpy as jnp
from jax import lax
from jax.sharding import PartitionSpec as P

SWEEPS = 6


relaxation = 0.125
damping = 1.0


def stacked_rows(factor):
    real_left = jnp.concatenate([factor[0], factor[1]], axis=1)
    imag_left = jnp.concatenate([factor[1], -factor[0]], axis=1)
    return jnp.swapaxes(jnp.stack([real_left, imag_left], axis=1), 2, 3)


def stacked_left(factor):
    real_left = jnp.concatenate([factor[0], factor[1]], axis=1)
    imag_left = jnp.concatenate([factor[1], -factor[0]], axis=1)
    return jnp.stack([real_left, imag_left], axis=2)


def stacked_right(trace):
    return jnp.concatenate([trace[0], trace[1]], axis=1)


def sweep_whole(scaled, solution, target):
    receivers = target.shape[-1]
    sources = target.shape[2]
    wide = jnp.concatenate([scaled[0], scaled[1]], axis=-1)
    for sweep in range(SWEEPS):
        narrow = solution.astype(jnp.bfloat16)
        stacked = jnp.concatenate([narrow[0], narrow[1]], axis=1)
        products = jnp.einsum("qjc,qcr->qjr", stacked, wide, preferred_element_type=jnp.float32)
        real_real = products[:, :sources, :receivers]
        real_imag = products[:, :sources, receivers:]
        imag_real = products[:, sources:, :receivers]
        imag_imag = products[:, sources:, receivers:]
        image = jnp.stack([real_real - imag_imag, real_imag + imag_real])
        solution = solution + relaxation * (target - image - damping * solution)
    return solution


def strip_partials(rows, shot_count, core_count, core_index, rows_each, tile, span):
    rows = rows.astype(jnp.bfloat16)
    doubled = jnp.concatenate([rows, rows], axis=-1)
    windows = []
    for k in range(shot_count):
        start = ((k * core_count + core_index) * rows_each // tile) * tile
        windows.append(lax.dynamic_slice_in_dim(doubled[k], start, span, axis=-1))
    return jnp.stack(windows).reshape(shot_count * rows_each, *rows.shape[2:4], span)


def rebuild_gram(strips, tiles, tile):
    freq_local = strips.shape[1]
    receivers = tiles * tile
    span = strips.shape[-1]
    padded = jnp.pad(strips, [(0, 0)] * 3 + [(0, receivers - span)])
    padded = padded.reshape(tiles, tile, freq_local, 2, receivers)
    upper = jnp.stack([jnp.roll(padded[a], a * tile, axis=-1) for a in range(tiles)])
    upper = jnp.transpose(upper, (3, 2, 0, 1, 4)).reshape(2, freq_local, receivers, receivers)
    mirror = jnp.swapaxes(upper, 2, 3)
    mirror = jnp.stack([mirror[0], -mirror[1]])
    row_tile = lax.broadcasted_iota(jnp.int32, (tiles, 1, tiles, 1), 0)
    col_tile = lax.broadcasted_iota(jnp.int32, (tiles, 1, tiles, 1), 2)
    direct = (col_tile - row_tile) % tiles <= tiles // 2
    shape6 = (2, freq_local, tiles, tile, tiles, tile)
    whole = jnp.where(direct, upper.reshape(shape6), mirror.reshape(shape6))
    return whole.reshape(upper.shape)


def per_device(downgoing, upgoing, source_order):
    shot_count = lax.axis_size("shot")
    core_count = lax.axis_size("sub")
    core_index = lax.axis_index("sub")
    receivers = downgoing.shape[3]
    freq_local = downgoing.shape[1]
    sources = source_order.shape[0]
    groups = shot_count * core_count
    source_local = sources // groups
    rows_each = receivers // groups
    tiles = 8 if groups % 8 == 0 else groups
    tile = receivers // tiles
    span = (tiles // 2 + 1) * tile

    right = stacked_right(downgoing)

    left = stacked_rows(downgoing).reshape(freq_local, 2, shot_count, core_count, rows_each, -1)
    left = lax.dynamic_slice_in_dim(left, core_index, 1, 3)[:, :, :, 0]
    gram_rows = jnp.einsum("qpkit,qto->kiqpo", left, right, preferred_element_type=jnp.float32)
    gram_part = strip_partials(gram_rows, shot_count, core_count, core_index, rows_each, tile, span)
    gram_strip = lax.psum_scatter(gram_part, "shot", scatter_dimension=0, tiled=True)

    corr_all = jnp.einsum(
        "qtpu,qto->uqpo", stacked_left(upgoing), right, preferred_element_type=jnp.float32
    )
    order_table = source_order.reshape(shot_count, core_count, source_local)
    own_order = lax.dynamic_slice_in_dim(order_table, core_index, 1, 1).reshape(-1)
    corr_part = jnp.take(corr_all, own_order, axis=0).astype(jnp.bfloat16)

    local_power = jnp.sum(jnp.square(downgoing.astype(jnp.float32)), axis=(0, 2, 3))
    gram_strip, corr_part, local_power = lax.optimization_barrier((gram_strip, corr_part, local_power))

    shot_index = lax.axis_index("shot")
    corr_blocks = corr_part.reshape(shot_count, source_local, *corr_part.shape[1:])
    corr = lax.dynamic_index_in_dim(corr_blocks, shot_index, 0, keepdims=False).astype(jnp.float32)
    for shift in range(1, shot_count):
        outgoing = lax.dynamic_index_in_dim(corr_blocks, (shot_index + shift) % shot_count, 0, keepdims=False)
        pairs = [(k, (k + shift) % shot_count) for k in range(shot_count)]
        corr = corr + lax.ppermute(outgoing, "shot", perm=pairs).astype(jnp.float32)

    across = lax.all_gather(gram_strip, "shot", axis=0, tiled=True)
    across = across.reshape(shot_count, rows_each, freq_local, 2, span)
    power = lax.psum(local_power, "shot") / receivers
    across, power = lax.optimization_barrier((across, power))
    power_wide = power[None, :, None, None]

    if core_count == 2:
        other = lax.ppermute(across, "sub", perm=[(0, 1), (1, 0)])
        first = jnp.where(core_index == 0, across, other)
        second = jnp.where(core_index == 0, other, across)
        strips = jnp.stack([first, second], axis=1)
    else:
        strips = lax.all_gather(across, "sub", axis=1, tiled=False)
    strips = strips.reshape(receivers, freq_local, 2, span)
    whole = rebuild_gram(strips, tiles, tile)

    target = jnp.transpose(corr, (2, 1, 0, 3)) / power_wide

    scaled = (whole.astype(jnp.float32) / power_wide).astype(jnp.bfloat16)
    solution = jnp.zeros((2, freq_local, source_local, receivers), jnp.float32)
    return sweep_whole(scaled, solution, target)


def solution(mesh):
    return jax.shard_map(
        per_device,
        mesh=mesh,
        in_specs=(
            P(None, "freq", ("grp", "shot"), None),
            P(None, "freq", ("grp", "shot"), None),
            P("grp"),
        ),
        out_specs=P(None, "freq", ("grp", "shot", "sub"), None),
        check_vma=False,
    )
```

```python
import jax
import jax.numpy as jnp
from jax import lax
from jax.sharding import PartitionSpec as P

SWEEPS = 6


relaxation = 0.125
damping = 1.0


def stacked_rows(factor):
    real_left = jnp.concatenate([factor[0], factor[1]], axis=1)
    imag_left = jnp.concatenate([factor[1], -factor[0]], axis=1)
    return jnp.swapaxes(jnp.stack([real_left, imag_left], axis=1), 2, 3)


def stacked_left(factor):
    real_left = jnp.concatenate([factor[0], factor[1]], axis=1)
    imag_left = jnp.concatenate([factor[1], -factor[0]], axis=1)
    return jnp.stack([real_left, imag_left], axis=2)


def stacked_right(trace):
    return jnp.concatenate([trace[0], trace[1]], axis=1)


def sweep_whole(scaled, solution, target):
    receivers = target.shape[-1]
    sources = target.shape[2]
    wide = jnp.concatenate([scaled[0], scaled[1]], axis=-1)
    for sweep in range(SWEEPS):
        narrow = solution.astype(jnp.bfloat16)
        stacked = jnp.concatenate([narrow[0], narrow[1]], axis=1)
        products = jnp.einsum("qjc,qcr->qjr", stacked, wide, preferred_element_type=jnp.float32)
        real_real = products[:, :sources, :receivers]
        real_imag = products[:, :sources, receivers:]
        imag_real = products[:, sources:, :receivers]
        imag_imag = products[:, sources:, receivers:]
        image = jnp.stack([real_real - imag_imag, real_imag + imag_real])
        solution = solution + relaxation * (target - image - damping * solution)
    return solution


def strip_partials(rows, shot_count, core_count, core_index, rows_each, tile, span):
    rows = rows.astype(jnp.bfloat16)
    doubled = jnp.concatenate([rows, rows], axis=-1)
    windows = []
    for k in range(shot_count):
        start = ((k * core_count + core_index) * rows_each // tile) * tile
        windows.append(lax.dynamic_slice_in_dim(doubled[k], start, span, axis=-1))
    return jnp.stack(windows).reshape(shot_count * rows_each, *rows.shape[2:4], span)


def rebuild_gram(strips, tiles, tile):
    freq_local = strips.shape[1]
    receivers = tiles * tile
    span = strips.shape[-1]
    padded = jnp.pad(strips, [(0, 0)] * 3 + [(0, receivers - span)])
    padded = padded.reshape(tiles, tile, freq_local, 2, receivers)
    upper = jnp.stack([jnp.roll(padded[a], a * tile, axis=-1) for a in range(tiles)])
    upper = jnp.transpose(upper, (3, 2, 0, 1, 4)).reshape(2, freq_local, receivers, receivers)
    mirror = jnp.swapaxes(upper, 2, 3)
    mirror = jnp.stack([mirror[0], -mirror[1]])
    row_tile = lax.broadcasted_iota(jnp.int32, (tiles, 1, tiles, 1), 0)
    col_tile = lax.broadcasted_iota(jnp.int32, (tiles, 1, tiles, 1), 2)
    direct = (col_tile - row_tile) % tiles <= tiles // 2
    shape6 = (2, freq_local, tiles, tile, tiles, tile)
    whole = jnp.where(direct, upper.reshape(shape6), mirror.reshape(shape6))
    return whole.reshape(upper.shape)


def per_device(downgoing, upgoing, source_order):
    shot_count = lax.axis_size("shot")
    core_count = lax.axis_size("sub")
    core_index = lax.axis_index("sub")
    receivers = downgoing.shape[3]
    freq_local = downgoing.shape[1]
    sources = source_order.shape[0]
    groups = shot_count * core_count
    source_local = sources // groups
    rows_each = receivers // groups
    tiles = 8 if groups % 8 == 0 else groups
    tile = receivers // tiles
    span = (tiles // 2 + 1) * tile

    right = stacked_right(downgoing)

    left = stacked_rows(downgoing).reshape(freq_local, 2, shot_count, core_count, rows_each, -1)
    left = lax.dynamic_slice_in_dim(left, core_index, 1, 3)[:, :, :, 0]
    gram_rows = jnp.einsum("qpkit,qto->kiqpo", left, right, preferred_element_type=jnp.float32)
    gram_part = strip_partials(gram_rows, shot_count, core_count, core_index, rows_each, tile, span)
    gram_strip = lax.psum_scatter(gram_part, "shot", scatter_dimension=0, tiled=True)

    corr_all = jnp.einsum(
        "qtpu,qto->uqpo", stacked_left(upgoing), right, preferred_element_type=jnp.float32
    )
    order_table = source_order.reshape(shot_count, core_count, source_local)
    own_order = lax.dynamic_slice_in_dim(order_table, core_index, 1, 1).reshape(-1)
    corr_part = jnp.take(corr_all, own_order, axis=0).astype(jnp.bfloat16)

    gram_strip, corr_part, power_trace = lax.optimization_barrier((gram_strip, corr_part, downgoing))

    shot_index = lax.axis_index("shot")
    corr_blocks = corr_part.reshape(shot_count, source_local, *corr_part.shape[1:])
    corr = lax.dynamic_index_in_dim(corr_blocks, shot_index, 0, keepdims=False).astype(jnp.float32)
    for shift in range(1, shot_count):
        outgoing = lax.dynamic_index_in_dim(corr_blocks, (shot_index + shift) % shot_count, 0, keepdims=False)
        pairs = [(k, (k + shift) % shot_count) for k in range(shot_count)]
        corr = corr + lax.ppermute(outgoing, "shot", perm=pairs).astype(jnp.float32)

    across = lax.all_gather(gram_strip, "shot", axis=0, tiled=True)
    across = across.reshape(shot_count, rows_each, freq_local, 2, span)
    local_power = jnp.sum(jnp.square(power_trace.astype(jnp.float32)), axis=(0, 2, 3))
    total_power = local_power
    for shift in range(1, shot_count):
        pairs = [(k, (k + shift) % shot_count) for k in range(shot_count)]
        total_power = total_power + lax.ppermute(local_power, "shot", perm=pairs)
    power = total_power / receivers
    across, power = lax.optimization_barrier((across, power))
    power_wide = power[None, :, None, None]

    if core_count == 2:
        other = lax.ppermute(across, "sub", perm=[(0, 1), (1, 0)])
        first = jnp.where(core_index == 0, across, other)
        second = jnp.where(core_index == 0, other, across)
        strips = jnp.stack([first, second], axis=1)
    else:
        strips = lax.all_gather(across, "sub", axis=1, tiled=False)
    strips = strips.reshape(receivers, freq_local, 2, span)
    whole = rebuild_gram(strips, tiles, tile)

    target = jnp.transpose(corr, (2, 1, 0, 3)) / power_wide

    scaled = (whole.astype(jnp.float32) / power_wide).astype(jnp.bfloat16)
    solution = jnp.zeros((2, freq_local, source_local, receivers), jnp.float32)
    return sweep_whole(scaled, solution, target)


def solution(mesh):
    return jax.shard_map(
        per_device,
        mesh=mesh,
        in_specs=(
            P(None, "freq", ("grp", "shot"), None),
            P(None, "freq", ("grp", "shot"), None),
            P("grp"),
        ),
        out_specs=P(None, "freq", ("grp", "shot", "sub"), None),
        check_vma=False,
    )
```

```python
import jax
import jax.numpy as jnp
from jax import lax
from jax.sharding import PartitionSpec as P

SWEEPS = 6


relaxation = 0.125
damping = 1.0


def stacked_rows(factor):
    real_left = jnp.concatenate([factor[0], factor[1]], axis=1)
    imag_left = jnp.concatenate([factor[1], -factor[0]], axis=1)
    return jnp.swapaxes(jnp.stack([real_left, imag_left], axis=1), 2, 3)


def stacked_left(factor):
    real_left = jnp.concatenate([factor[0], factor[1]], axis=1)
    imag_left = jnp.concatenate([factor[1], -factor[0]], axis=1)
    return jnp.stack([real_left, imag_left], axis=2)


def stacked_right(trace):
    return jnp.concatenate([trace[0], trace[1]], axis=1)


def sweep_whole(scaled, solution, target):
    receivers = target.shape[-1]
    sources = target.shape[2]
    wide = jnp.concatenate([scaled[0], scaled[1]], axis=-1)
    for sweep in range(SWEEPS):
        narrow = solution.astype(jnp.bfloat16)
        stacked = jnp.concatenate([narrow[0], narrow[1]], axis=1)
        products = jnp.einsum("qjc,qcr->qjr", stacked, wide, preferred_element_type=jnp.float32)
        real_real = products[:, :sources, :receivers]
        real_imag = products[:, :sources, receivers:]
        imag_real = products[:, sources:, :receivers]
        imag_imag = products[:, sources:, receivers:]
        image = jnp.stack([real_real - imag_imag, real_imag + imag_real])
        solution = solution + relaxation * (target - image - damping * solution)
    return solution


def strip_partials(rows, shot_count, core_count, core_index, rows_each, tile, span):
    rows = rows.astype(jnp.bfloat16)
    doubled = jnp.concatenate([rows, rows], axis=-1)
    windows = []
    for k in range(shot_count):
        start = ((k * core_count + core_index) * rows_each // tile) * tile
        windows.append(lax.dynamic_slice_in_dim(doubled[k], start, span, axis=-1))
    return jnp.stack(windows).reshape(shot_count * rows_each, *rows.shape[2:4], span)


def rebuild_gram(strips, tiles, tile):
    freq_local = strips.shape[1]
    receivers = tiles * tile
    span = strips.shape[-1]
    padded = jnp.pad(strips, [(0, 0)] * 3 + [(0, receivers - span)])
    padded = padded.reshape(tiles, tile, freq_local, 2, receivers)
    upper = jnp.stack([jnp.roll(padded[a], a * tile, axis=-1) for a in range(tiles)])
    upper = jnp.transpose(upper, (3, 2, 0, 1, 4)).reshape(2, freq_local, receivers, receivers)
    mirror = jnp.swapaxes(upper, 2, 3)
    mirror = jnp.stack([mirror[0], -mirror[1]])
    row_tile = lax.broadcasted_iota(jnp.int32, (tiles, 1, tiles, 1), 0)
    col_tile = lax.broadcasted_iota(jnp.int32, (tiles, 1, tiles, 1), 2)
    direct = (col_tile - row_tile) % tiles <= tiles // 2
    shape6 = (2, freq_local, tiles, tile, tiles, tile)
    whole = jnp.where(direct, upper.reshape(shape6), mirror.reshape(shape6))
    return whole.reshape(upper.shape)


def per_device(downgoing, upgoing, source_order):
    shot_count = lax.axis_size("shot")
    core_count = lax.axis_size("sub")
    core_index = lax.axis_index("sub")
    receivers = downgoing.shape[3]
    freq_local = downgoing.shape[1]
    sources = source_order.shape[0]
    groups = shot_count * core_count
    source_local = sources // groups
    rows_each = receivers // groups
    tiles = 8 if groups % 8 == 0 else groups
    tile = receivers // tiles
    span = (tiles // 2 + 1) * tile

    right = stacked_right(downgoing)

    left = stacked_rows(downgoing).reshape(freq_local, 2, shot_count, core_count, rows_each, -1)
    left = lax.dynamic_slice_in_dim(left, core_index, 1, 3)[:, :, :, 0]
    gram_rows = jnp.einsum("qpkit,qto->kiqpo", left, right, preferred_element_type=jnp.float32)
    gram_part = strip_partials(gram_rows, shot_count, core_count, core_index, rows_each, tile, span)
    gram_strip = lax.psum_scatter(gram_part, "shot", scatter_dimension=0, tiled=True)

    corr_all = jnp.einsum(
        "qtpu,qto->uqpo", stacked_left(upgoing), right, preferred_element_type=jnp.float32
    )
    order_table = source_order.reshape(shot_count, core_count, source_local)
    own_order = lax.dynamic_slice_in_dim(order_table, core_index, 1, 1).reshape(-1)
    corr_part = jnp.take(corr_all, own_order, axis=0).astype(jnp.bfloat16)

    gram_strip, corr_part, power_trace = lax.optimization_barrier((gram_strip, corr_part, downgoing))

    shot_index = lax.axis_index("shot")
    corr_blocks = corr_part.reshape(shot_count, source_local, *corr_part.shape[1:])
    corr = lax.dynamic_index_in_dim(corr_blocks, shot_index, 0, keepdims=False).astype(jnp.float32)
    outgoing = [
        lax.dynamic_index_in_dim(corr_blocks, (shot_index + shift) % shot_count, 0, keepdims=False)
        for shift in range(1, shot_count)
    ]

    across = lax.all_gather(gram_strip, "shot", axis=0, tiled=True)
    across = across.reshape(shot_count, rows_each, freq_local, 2, span)
    local_power = jnp.sum(jnp.square(power_trace.astype(jnp.float32)), axis=(0, 2, 3))
    power = lax.psum(local_power, "shot") / receivers
    across, power, outgoing = lax.optimization_barrier((across, power, outgoing))
    for shift in range(1, shot_count):
        pairs = [(k, (k + shift) % shot_count) for k in range(shot_count)]
        corr = corr + lax.ppermute(outgoing[shift - 1], "shot", perm=pairs).astype(jnp.float32)
    power_wide = power[None, :, None, None]

    if core_count == 2:
        other = lax.ppermute(across, "sub", perm=[(0, 1), (1, 0)])
        first = jnp.where(core_index == 0, across, other)
        second = jnp.where(core_index == 0, other, across)
        strips = jnp.stack([first, second], axis=1)
    else:
        strips = lax.all_gather(across, "sub", axis=1, tiled=False)
    strips = strips.reshape(receivers, freq_local, 2, span)
    whole = rebuild_gram(strips, tiles, tile)

    target = jnp.transpose(corr, (2, 1, 0, 3)) / power_wide

    scaled = (whole.astype(jnp.float32) / power_wide).astype(jnp.bfloat16)
    solution = jnp.zeros((2, freq_local, source_local, receivers), jnp.float32)
    return sweep_whole(scaled, solution, target)


def solution(mesh):
    return jax.shard_map(
        per_device,
        mesh=mesh,
        in_specs=(
            P(None, "freq", ("grp", "shot"), None),
            P(None, "freq", ("grp", "shot"), None),
            P("grp"),
        ),
        out_specs=P(None, "freq", ("grp", "shot", "sub"), None),
        check_vma=False,
    )
```
